256 devices in a mesh: src: 8 (over z_hi, y), width: 32 (over z_lo, x, core).
Axes of the slice: x: 4, y: 4, z: 8 (z_hi: 2, z_lo: 4; z = z_hi * 4 + z_lo), core: 2. Of those that a mesh axis runs over, the one named last changes fastest.
Arguments:
- resid: bfloat16 [8, 512, 8192], P('src', None, 'width'), may hold values from -6 to 6
- enc_w: bfloat16 [8, 8192, 6144], P('src', 'width'), may hold values from -0.0625 to 0.0625
- enc_b: float32 [8, 6144], P('src'), may hold values from -3 to 3
- dec_w: bfloat16 [8, 6144, 8192], P('src', None, 'width'), may hold values from -0.078125 to 0.078125
- target: bfloat16 [512, 8192], P(None, 'width'), may hold values from -36 to 36
- norm_gain: float32 [8192], P('width'), may hold values from 0.5 to 1.5
- wq: bfloat16 [8192, 8192], P(None, 'width'), may hold values from -0.0625 to 0.0625
- wk: bfloat16 [8192, 1024], P('width'), may hold values from -0.0625 to 0.0625
- wv: bfloat16 [8192, 1024], P('width'), may hold values from -0.0625 to 0.0625
- prompt_ids: int32 [512], replicated, may hold values from 0 to 3, never falling along the last dimension, each value on 1 to 256 neighbouring positions
Outputs:
- mlp_out: bfloat16 [512, 8192], P('src', 'width')
- context: bfloat16 [512, 8192], P('src', 'width')
The draws below stay inside these ranges and needn't reach their ends.
Inputs may be any that keep to these rules, and one draw needn't show every extreme that they name: `prompt_ids`: rows of one prompt are contiguous and numbered in increasing order; the longest prompt has 256 rows.
All inputs are finite; a program needn't handle non-finite values.
Results may differ from the reference program's by a relative error of at most 0.008.
Values may be sent and summed in bfloat16 or wider, within the bound.
No kernel may reach another device: no remote copies, remote signals or barrier semaphores. Data moves between devices by JAX's collectives and lax.ppermute only.
A program may use at most 128 MiB of HBM per device.

```python
import math
import jax
import jax.numpy as jnp
import numpy as np
from jax import lax

D = 8192
HD = 128
GROUP = 8
F = 6144
ROWS = 512
LAYERS = 8
HEADS = 64
KV = 8


def draw_target(key, part):
    first, second = jax.random.split(key, 2)
    columns = 1.0 + 2.0 * jnp.arange(D, dtype=jnp.float32) / D
    row_scale = jnp.exp(jax.random.uniform(second, (ROWS, 1), jnp.float32, math.log(0.3), math.log(3.0)))
    base = jnp.clip(jax.random.normal(first, (ROWS, D), jnp.float32), -4.0, 4.0)
    return (base * columns[None, :] * row_scale).astype(jnp.bfloat16)


def steps_of(rng, dims, cuts, least, largest):
    factor_of, own = 1.0, jax.random.fold_in(rng, 6)
    for axis_at, parts in cuts:
        steps = jnp.exp(jax.random.uniform(jax.random.fold_in(own, axis_at), (parts,), jnp.float32, least / len(cuts), largest / len(cuts)))
        factor_of = factor_of * jnp.repeat(steps, dims[axis_at] // parts).reshape([-1 if axis == axis_at else 1 for axis in range(len(dims))])
    return factor_of


def profile(number_of, total, limit, lean):
    portions = [(1 << 20) // math.isqrt(rank ** lean) + 1 for rank in range(2, number_of + 1)]
    spare, given = total - limit - (number_of - 1), [1] * (number_of - 1)
    while spare > 0:
        movable = [i for i in range(number_of - 1) if given[i] < limit]
        pool, remaining = sum([portions[i] for i in movable]), spare
        for i in movable:
            addition = min(limit - given[i], max(1, remaining * portions[i] // pool), spare)
            given[i] = given[i] + addition
            spare = spare - addition
    return np.array([limit] + given)


def ragged(key, number_of, total, reach, slope):
    if number_of == 2:
        one = jax.random.randint(key, (), max(1, total - reach), min(reach, total - 1) + 1)
        return jnp.stack([one, total - one])
    sizes = jnp.asarray(profile(number_of, total, reach, slope), jnp.int32)
    twos = (number_of - 1) // 2
    source_of, taker = sizes[1:1 + 2 * twos:2], sizes[2:2 + 2 * twos:2]
    margin = jnp.minimum(source_of - 1, reach - taker)
    moved = jax.random.randint(jax.random.fold_in(key, 1), (twos,), 0, 1 << 20) % (margin + 1)
    sizes = sizes.at[1:1 + 2 * twos:2].set(source_of - moved).at[2:2 + 2 * twos:2].set(taker + moved)
    return sizes[jax.random.permutation(jax.random.fold_in(key, 2), number_of)]


def gaussian(rng, extent, deviation, limit, shards=(), held_as=jnp.bfloat16):
    loudness = steps_of(rng, extent, shards, -0.22, 0.18) if shards else 1.0
    drawn = jax.random.normal(rng, extent, jnp.float32) * deviation * loudness
    return jnp.minimum(jnp.maximum(drawn, -limit), limit).astype(held_as)


def setup_inputs(seed: int = 0) -> dict:
    key_of = jax.random.split(jax.random.key(seed), 11)
    resid = gaussian(key_of[0], (LAYERS, ROWS, D), 1.0, 6.0, ((0, 8), (2, 32)))
    enc_w = gaussian(key_of[1], (LAYERS, D, F), D ** -0.5, 0.0625, ((0, 8), (1, 32)))
    enc_b = gaussian(key_of[2], (LAYERS, F), 0.5, 3.0, ((0, 8),), jnp.float32)
    dec_w = gaussian(key_of[3], (LAYERS, F, D), F ** -0.5, 0.078125, ((0, 8), (2, 32)))
    target = draw_target(jax.random.fold_in(key_of[10], 71), 0)
    norm_gain = jnp.clip(0.5 + 1.0 * jax.random.uniform(key_of[5], (D,), jnp.float32) ** steps_of(key_of[5], (D,), ((0, 32),), -0.2, 0.2), 0.5, 1.5)
    wq = gaussian(key_of[6], (D, HEADS * HD), D ** -0.5, 0.0625, ((1, 32),))
    wk = gaussian(key_of[7], (D, KV * HD), D ** -0.5, 0.0625, ((0, 32),))
    wv = gaussian(key_of[8], (D, KV * HD), D ** -0.5, 0.0625, ((0, 32),))
    prompt_ids = jnp.searchsorted(jnp.cumsum(ragged(key_of[9], max(ROWS // 128, 4), ROWS, ROWS // 2, 2)), jnp.arange(ROWS), side="right").astype(jnp.int32)
    return {"resid": resid, "enc_w": enc_w, "enc_b": enc_b, "dec_w": dec_w, "target": target, "norm_gain": norm_gain, "wq": wq, "wk": wk, "wv": wv, "prompt_ids": prompt_ids}


def reference(resid, enc_w, enc_b, dec_w, target, norm_gain, wq, wk, wv, prompt_ids):

    def layer_step(total, inputs):
        rows, w_enc, bias, w_dec = inputs
        pre = jnp.dot(rows, w_enc, preferred_element_type=jnp.float32)
        feats = jnp.maximum(pre + bias[None, :], 0.0).astype(jnp.bfloat16)
        return (total + jnp.dot(feats, w_dec, preferred_element_type=jnp.float32), None)
    mlp, _ = lax.scan(layer_step, jnp.zeros((ROWS, D), jnp.float32), (resid, enc_w, enc_b, dec_w))
    mlp_out = mlp.astype(jnp.bfloat16)
    stream = target.astype(jnp.float32) + mlp
    power = lax.optimization_barrier(jnp.mean(stream * stream, axis=1, keepdims=True))
    normed = (stream * lax.rsqrt(power + 1e-05) * norm_gain[None, :]).astype(jnp.bfloat16)
    query = jnp.dot(normed, wq, preferred_element_type=jnp.float32).astype(jnp.bfloat16)
    keys = jnp.dot(normed, wk, preferred_element_type=jnp.float32).astype(jnp.bfloat16)
    values = jnp.dot(normed, wv, preferred_element_type=jnp.float32).astype(jnp.bfloat16)
    index = jnp.arange(ROWS, dtype=jnp.int32)
    allowed = (prompt_ids[:, None] == prompt_ids[None, :]) & (index[None, :] <= index[:, None])
    query4 = query.reshape(ROWS, KV, GROUP, HD).astype(jnp.float32)
    keys3 = keys.reshape(ROWS, KV, HD).astype(jnp.float32)
    values3 = values.reshape(ROWS, KV, HD).astype(jnp.float32)
    scores = jnp.einsum('qkgd,skd->kgqs', query4, keys3) / math.sqrt(HD)
    scores = jnp.where(allowed[None, None], scores, -1e+30)
    peak = lax.optimization_barrier(jnp.max(scores, axis=-1, keepdims=True))
    weights = jnp.exp(scores - peak)
    probs = (weights / lax.optimization_barrier(jnp.sum(weights, axis=-1, keepdims=True))).astype(jnp.bfloat16)
    context = jnp.einsum('kgqs,skd->qkgd', probs.astype(jnp.float32), values3)
    return (mlp_out, context.reshape(ROWS, HEADS * HD).astype(jnp.bfloat16))
```

```python
import math

import jax
import jax.numpy as jnp
from jax import lax
from jax.sharding import Mesh
from jax.sharding import PartitionSpec as P

HD = 128
GROUP = 8
WIDTH = ("wc", "core")
SWAP = [(0, 1), (1, 0)]


def contract0(a, b):
    return lax.dot_general(a, b, (((0,), (0,)), ((), ())), preferred_element_type=jnp.float32)


def on_device(resid, enc_w, enc_b, dec_w, target, norm_gain, wq, wk, wv, prompt_ids):
    n_wc = lax.axis_size("wc")
    n_core = lax.axis_size("core")
    n_src = lax.axis_size("src")
    core = lax.axis_index("core")
    chip = lax.axis_index("wc")
    src = lax.axis_index("src")
    width_pos = chip * n_core + core
    rows_all = resid.shape[1]
    width_local = resid.shape[2]
    width_all = width_local * n_wc * n_core
    feats_all = enc_w.shape[2]
    half = feats_all // 2
    share = half // n_wc
    other = 1 - core

    x = resid[0]
    we = enc_w[0]
    we_mine = lax.dynamic_slice_in_dim(we, core * half, half, 1)
    we_give = lax.dynamic_slice_in_dim(we, other * half, half, 1)
    we_got = lax.ppermute(we_give, "core", SWAP)
    x_got = lax.ppermute(x, "core", SWAP)
    pre = lax.dot_general(we_mine, x, (((0,), (1,)), ((), ())), preferred_element_type=jnp.float32)
    pre = pre + lax.dot_general(we_got, x_got, (((0,), (1,)), ((), ())), preferred_element_type=jnp.float32)
    pre_share = lax.psum_scatter(pre, "wc", scatter_dimension=0, tiled=True)
    bias = lax.dynamic_slice_in_dim(enc_b[0], core * half + chip * share, share, 0)
    feats_t = jnp.maximum(pre_share + bias[:, None], 0.0).astype(jnp.bfloat16)
    feats_half = lax.all_gather(feats_t, "wc", axis=0, tiled=True)

    wd = dec_w[0]
    wd_mine = lax.dynamic_slice_in_dim(wd, core * half, half, 0)
    wd_give = lax.dynamic_slice_in_dim(wd, other * half, half, 0)
    wd_got = lax.ppermute(wd_give, "core", SWAP)
    part_mine = contract0(feats_half, wd_mine)
    part_other = contract0(feats_half, wd_got)
    mlp_layer = part_mine + lax.ppermute(part_other, "core", SWAP)

    query_rows = rows_all // n_src
    row_start = src * query_rows
    mlp = lax.psum_scatter(mlp_layer, "src", scatter_dimension=0, tiled=True)
    mlp_out = mlp.astype(jnp.bfloat16)
    tgt = lax.dynamic_slice_in_dim(target, row_start, query_rows, 0)
    stream = tgt.astype(jnp.float32) + mlp
    stream_full = lax.all_gather(stream, WIDTH, axis=1, tiled=True)
    gain_full = lax.all_gather(norm_gain, WIDTH, axis=0, tiled=True)
    power = jnp.sum(stream_full * stream_full, axis=1) / width_all
    scale = lax.rsqrt(power + 1e-05)[:, None]
    normed_full = (stream_full * scale * gain_full[None, :]).astype(jnp.bfloat16)
    normed_loc = (stream * scale * norm_gain[None, :]).astype(jnp.bfloat16)

    query = jnp.dot(normed_full, wq, preferred_element_type=jnp.float32).astype(jnp.bfloat16)
    key_part = jnp.dot(normed_loc, wk, preferred_element_type=jnp.float32)
    value_part = jnp.dot(normed_loc, wv, preferred_element_type=jnp.float32)
    key_total, value_total = lax.psum((key_part, value_part), WIDTH)
    heads_here = wq.shape[1] // HD
    kv_index = width_pos * heads_here // GROUP
    key_head = lax.dynamic_slice_in_dim(key_total, kv_index * HD, HD, 1).astype(jnp.bfloat16)
    value_head = lax.dynamic_slice_in_dim(value_total, kv_index * HD, HD, 1).astype(jnp.bfloat16)
    key_head = lax.all_gather(key_head, "src", axis=0, tiled=True)
    value_head = lax.all_gather(value_head, "src", axis=0, tiled=True)

    query3 = query.reshape(query_rows, heads_here, HD)
    scores = jnp.einsum(
        "qhd,sd->hqs", query3, key_head, preferred_element_type=jnp.float32
    ) / math.sqrt(HD)
    query_index = row_start + jnp.arange(query_rows, dtype=jnp.int32)
    key_index = jnp.arange(rows_all, dtype=jnp.int32)
    query_prompt = lax.dynamic_slice_in_dim(prompt_ids, row_start, query_rows, 0)
    allowed = (query_prompt[:, None] == prompt_ids[None, :]) & (
        key_index[None, :] <= query_index[:, None]
    )
    scores = jnp.where(allowed[None], scores, -1e30)
    peak = jnp.max(scores, axis=-1, keepdims=True)
    weights = jnp.exp(scores - peak)
    probs = (weights / jnp.sum(weights, axis=-1, keepdims=True)).astype(jnp.bfloat16)
    context = jnp.einsum("hqs,sd->qhd", probs, value_head, preferred_element_type=jnp.float32)
    return (mlp_out, context.reshape(query_rows, heads_here * HD).astype(jnp.bfloat16))


def solution(mesh):
    n_src = mesh.shape["src"]
    n_width = mesh.shape["width"]
    fine = Mesh(mesh.devices.reshape(n_src, n_width // 2, 2), ("src", "wc", "core"))
    in_specs = (
        P("src", None, WIDTH),
        P("src", WIDTH, None),
        P("src", None),
        P("src", None, WIDTH),
        P(None, WIDTH),
        P(WIDTH),
        P(None, WIDTH),
        P(WIDTH, None),
        P(WIDTH, None),
        P(),
    )
    out_specs = (P("src", WIDTH), P("src", WIDTH))
    return jax.shard_map(
        on_device, mesh=fine, in_specs=in_specs, out_specs=out_specs, check_vma=False
    )
```

```python
import math

import jax
import jax.numpy as jnp
from jax import lax
from jax.sharding import Mesh
from jax.sharding import PartitionSpec as P

HD = 128
GROUP = 8
WIDTH = ("wch", "wcl", "core")
CHIP = ("wch", "wcl")
SWAP = [(0, 1), (1, 0)]


def contract0(a, b):
    return lax.dot_general(a, b, (((0,), (0,)), ((), ())), preferred_element_type=jnp.float32)


def on_device(resid, enc_w, enc_b, dec_w, target, norm_gain, wq, wk, wv, prompt_ids):
    n_chip = lax.axis_size(CHIP)
    n_core = lax.axis_size("core")
    n_src = lax.axis_size("src")
    core = lax.axis_index("core")
    chip = lax.axis_index(CHIP)
    src = lax.axis_index("src")
    width_pos = chip * n_core + core
    rows_all = resid.shape[1]
    width_local = resid.shape[2]
    width_all = width_local * n_chip * n_core
    feats_all = enc_w.shape[2]
    share = feats_all // (n_chip * n_core)
    other = 1 - core

    x = resid[0]
    we = enc_w[0].reshape(width_local, n_chip, n_core, share)
    we_mine = lax.dynamic_index_in_dim(we, core, 2, keepdims=False).reshape(width_local, n_chip * share)
    we_give = lax.dynamic_index_in_dim(we, other, 2, keepdims=False).reshape(width_local, n_chip * share)
    we_got = lax.ppermute(we_give, "core", SWAP)
    x_got = lax.ppermute(x, "core", SWAP)
    pre = lax.dot_general(we_mine, x, (((0,), (1,)), ((), ())), preferred_element_type=jnp.float32)
    pre = pre + lax.dot_general(we_got, x_got, (((0,), (1,)), ((), ())), preferred_element_type=jnp.float32)
    pre_share = lax.psum_scatter(pre, CHIP, scatter_dimension=0, tiled=True)
    bias = lax.dynamic_slice_in_dim(enc_b[0], width_pos * share, share, 0)
    feats_t = jnp.maximum(pre_share + bias[:, None], 0.0).astype(jnp.bfloat16)
    feats = lax.all_gather(feats_t, WIDTH, axis=0, tiled=True)
    mlp_layer = contract0(feats, dec_w[0])

    query_rows = rows_all // n_src
    row_start = src * query_rows
    mlp = lax.psum_scatter(mlp_layer, "src", scatter_dimension=0, tiled=True)
    mlp_out = mlp.astype(jnp.bfloat16)
    tgt = lax.dynamic_slice_in_dim(target, row_start, query_rows, 0)
    stream = tgt.astype(jnp.float32) + mlp
    packed = jnp.concatenate([stream, norm_gain[None, :]], axis=0)
    packed_full = lax.all_gather(packed, WIDTH, axis=1, tiled=True)
    stream_full = packed_full[:query_rows]
    gain_full = packed_full[query_rows]
    power = jnp.sum(stream_full * stream_full, axis=1) / width_all
    scale = lax.rsqrt(power + 1e-05)[:, None]
    normed_full = (stream_full * scale * gain_full[None, :]).astype(jnp.bfloat16)
    normed_loc = (stream * scale * norm_gain[None, :]).astype(jnp.bfloat16)

    query = jnp.dot(normed_full, wq, preferred_element_type=jnp.float32).astype(jnp.bfloat16)
    n_kv = wk.shape[1] // HD
    key_part = jnp.dot(normed_loc, wk, preferred_element_type=jnp.float32).reshape(query_rows, n_kv, 1, HD)
    value_part = jnp.dot(normed_loc, wv, preferred_element_type=jnp.float32).reshape(query_rows, n_kv, 1, HD)
    kv_part = jnp.concatenate([key_part, value_part], axis=2).reshape(query_rows, n_kv * 2 * HD)
    kv_share = lax.psum_scatter(kv_part, WIDTH, scatter_dimension=1, tiled=True).astype(jnp.bfloat16)
    kv_all = lax.all_gather(kv_share, ("src", "wcl", "core"), axis=0, tiled=False)
    quarter = kv_share.shape[1]
    kv_all = kv_all.reshape(n_src, -1, query_rows, quarter).transpose(0, 2, 1, 3).reshape(rows_all, -1)
    key_head = kv_all[:, :HD]
    value_head = kv_all[:, HD:]
    heads_here = wq.shape[1] // HD

    query3 = query.reshape(query_rows, heads_here, HD)
    scores = jnp.einsum(
        "qhd,sd->hqs", query3, key_head, preferred_element_type=jnp.float32
    ) / math.sqrt(HD)
    query_index = row_start + jnp.arange(query_rows, dtype=jnp.int32)
    key_index = jnp.arange(rows_all, dtype=jnp.int32)
    query_prompt = lax.dynamic_slice_in_dim(prompt_ids, row_start, query_rows, 0)
    allowed = (query_prompt[:, None] == prompt_ids[None, :]) & (
        key_index[None, :] <= query_index[:, None]
    )
    scores = jnp.where(allowed[None], scores, -1e30)
    peak = jnp.max(scores, axis=-1, keepdims=True)
    weights = jnp.exp(scores - peak)
    probs = (weights / jnp.sum(weights, axis=-1, keepdims=True)).astype(jnp.bfloat16)
    context = jnp.einsum("hqs,sd->qhd", probs, value_head, preferred_element_type=jnp.float32)
    return (mlp_out, context.reshape(query_rows, heads_here * HD).astype(jnp.bfloat16))


def solution(mesh):
    n_src = mesh.shape["src"]
    n_width = mesh.shape["width"]
    fine = Mesh(mesh.devices.reshape(n_src, n_width // 4, 2, 2), ("src", "wch", "wcl", "core"))
    in_specs = (
        P("src", None, WIDTH),
        P("src", WIDTH, None),
        P("src", None),
        P("src", None, WIDTH),
        P(None, WIDTH),
        P(WIDTH),
        P(None, WIDTH),
        P(WIDTH, None),
        P(WIDTH, None),
        P(),
    )
    out_specs = (P("src", WIDTH), P("src", WIDTH))
    return jax.shard_map(
        on_device, mesh=fine, in_specs=in_specs, out_specs=out_specs, check_vma=False
    )
```

```python
import math

import jax
import jax.numpy as jnp
from jax import lax
from jax.sharding import Mesh
from jax.sharding import PartitionSpec as P

HD = 128
GROUP = 8
WIDTH = ("wch", "wcl", "core")
CHIP = ("wch", "wcl")
SWAP = [(0, 1), (1, 0)]


def contract0(a, b):
    return lax.dot_general(a, b, (((0,), (0,)), ((), ())), preferred_element_type=jnp.float32)


def exchange_sum(blocks, axis, n, me):
    total = lax.dynamic_index_in_dim(blocks, me, 0, keepdims=False)
    for shift in range(1, n):
        piece = lax.dynamic_index_in_dim(blocks, (me + shift) % n, 0, keepdims=False)
        total = total + lax.ppermute(piece, axis, [(i, (i + shift) % n) for i in range(n)])
    return total


def exchange_gather(piece, axis, n, me):
    got = [None] * n
    got[0] = piece
    for shift in range(1, n):
        got[shift] = lax.ppermute(piece, axis, [(i, (i + shift) % n) for i in range(n)])
    stacked = jnp.stack(got)
    order = (me - jnp.arange(n)) % n
    return jnp.take(stacked, order, axis=0)


def on_device(resid, enc_w, enc_b, dec_w, target, norm_gain, wq, wk, wv, prompt_ids):
    n_chip = lax.axis_size(CHIP)
    n_core = lax.axis_size("core")
    n_src = lax.axis_size("src")
    core = lax.axis_index("core")
    chip = lax.axis_index(CHIP)
    src = lax.axis_index("src")
    width_pos = chip * n_core + core
    rows_all = resid.shape[1]
    width_local = resid.shape[2]
    width_all = width_local * n_chip * n_core
    feats_all = enc_w.shape[2]
    share = feats_all // (n_chip * n_core)
    other = 1 - core

    x = resid[0]
    we = enc_w[0].reshape(width_local, n_chip, n_core, share)
    we_mine = lax.dynamic_index_in_dim(we, core, 2, keepdims=False).reshape(width_local, n_chip * share)
    we_give = lax.dynamic_index_in_dim(we, other, 2, keepdims=False).reshape(width_local, n_chip * share)
    we_got = lax.ppermute(we_give, "core", SWAP)
    x_got = lax.ppermute(x, "core", SWAP)
    pre = lax.dot_general(we_mine, x, (((0,), (1,)), ((), ())), preferred_element_type=jnp.float32)
    pre = pre + lax.dot_general(we_got, x_got, (((0,), (1,)), ((), ())), preferred_element_type=jnp.float32)
    pre_share = lax.psum_scatter(pre, CHIP, scatter_dimension=0, tiled=True)
    bias = lax.dynamic_slice_in_dim(enc_b[0], width_pos * share, share, 0)
    feats_t = jnp.maximum(pre_share + bias[:, None], 0.0).astype(jnp.bfloat16)
    feats = lax.all_gather(feats_t, WIDTH, axis=0, tiled=True)
    mlp_layer = contract0(feats, dec_w[0])

    query_rows = rows_all // n_src
    row_start = src * query_rows
    mlp = exchange_sum(mlp_layer.reshape(n_src, query_rows, width_local), "src", n_src, src)
    mlp_out = mlp.astype(jnp.bfloat16)
    tgt = lax.dynamic_slice_in_dim(target, row_start, query_rows, 0)
    stream = tgt.astype(jnp.float32) + mlp
    packed = jnp.concatenate([stream, norm_gain[None, :]], axis=0)
    packed_full = lax.all_gather(packed, WIDTH, axis=1, tiled=True)
    stream_full = packed_full[:query_rows]
    gain_full = packed_full[query_rows]
    power = jnp.sum(stream_full * stream_full, axis=1) / width_all
    scale = lax.rsqrt(power + 1e-05)[:, None]
    normed_full = (stream_full * scale * gain_full[None, :]).astype(jnp.bfloat16)
    normed_loc = (stream * scale * norm_gain[None, :]).astype(jnp.bfloat16)

    query = jnp.dot(normed_full, wq, preferred_element_type=jnp.float32).astype(jnp.bfloat16)
    n_kv = wk.shape[1] // HD
    key_part = jnp.dot(normed_loc, wk, preferred_element_type=jnp.float32).reshape(query_rows, n_kv, 1, HD)
    value_part = jnp.dot(normed_loc, wv, preferred_element_type=jnp.float32).reshape(query_rows, n_kv, 1, HD)
    kv_part = jnp.concatenate([key_part, value_part], axis=2).reshape(query_rows, n_kv * 2 * HD)
    n_width = n_chip * n_core
    quarter = kv_part.shape[1] // n_width
    kv_blocks = kv_part.reshape(query_rows, n_width, quarter).transpose(1, 0, 2)
    kv_share = exchange_sum(kv_blocks, WIDTH, n_width, width_pos).astype(jnp.bfloat16)
    team = ("src", "wcl", "core")
    kv_all = exchange_gather(kv_share, team, n_src * 4, src * 4 + lax.axis_index("wcl") * 2 + core)
    kv_all = kv_all.reshape(n_src, -1, query_rows, quarter).transpose(0, 2, 1, 3).reshape(rows_all, -1)
    key_head = kv_all[:, :HD]
    value_head = kv_all[:, HD:]
    heads_here = wq.shape[1] // HD

    query3 = query.reshape(query_rows, heads_here, HD)
    scores = jnp.einsum(
        "qhd,sd->hqs", query3, key_head, preferred_element_type=jnp.float32
    ) / math.sqrt(HD)
    query_index = row_start + jnp.arange(query_rows, dtype=jnp.int32)
    key_index = jnp.arange(rows_all, dtype=jnp.int32)
    query_prompt = lax.dynamic_slice_in_dim(prompt_ids, row_start, query_rows, 0)
    allowed = (query_prompt[:, None] == prompt_ids[None, :]) & (
        key_index[None, :] <= query_index[:, None]
    )
    scores = jnp.where(allowed[None], scores, -1e30)
    peak = jnp.max(scores, axis=-1, keepdims=True)
    weights = jnp.exp(scores - peak)
    probs = (weights / jnp.sum(weights, axis=-1, keepdims=True)).astype(jnp.bfloat16)
    context = jnp.einsum("hqs,sd->qhd", probs, value_head, preferred_element_type=jnp.float32)
    return (mlp_out, context.reshape(query_rows, heads_here * HD).astype(jnp.bfloat16))


def solution(mesh):
    n_src = mesh.shape["src"]
    n_width = mesh.shape["width"]
    fine = Mesh(mesh.devices.reshape(n_src, n_width // 4, 2, 2), ("src", "wch", "wcl", "core"))
    in_specs = (
        P("src", None, WIDTH),
        P("src", WIDTH, None),
        P("src", None),
        P("src", None, WIDTH),
        P(None, WIDTH),
        P(WIDTH),
        P(None, WIDTH),
        P(WIDTH, None),
        P(WIDTH, None),
        P(),
    )
    out_specs = (P("src", WIDTH), P("src", WIDTH))
    return jax.shard_map(
        on_device, mesh=fine, in_specs=in_specs, out_specs=out_specs, check_vma=False
    )
```

```python
import math

import jax
import jax.numpy as jnp
from jax import lax
from jax.sharding import Mesh
from jax.sharding import PartitionSpec as P

HD = 128
GROUP = 8
WIDTH = ("wch", "wcl", "core")
CHIP = ("wch", "wcl")
SWAP = [(0, 1), (1, 0)]


def contract0(a, b):
    return lax.dot_general(a, b, (((0,), (0,)), ((), ())), preferred_element_type=jnp.float32)


def exchange_sum(blocks, axis, n, me):
    total = lax.dynamic_index_in_dim(blocks, me, 0, keepdims=False)
    for shift in range(1, n):
        piece = lax.dynamic_index_in_dim(blocks, (me + shift) % n, 0, keepdims=False)
        total = total + lax.ppermute(piece, axis, [(i, (i + shift) % n) for i in range(n)])
    return total


def halving_sum(blocks, axis, n, me):
    bits = n.bit_length() - 1
    rest = blocks.shape[1:]
    cur = blocks.reshape((2,) * bits + rest)
    for b in range(bits):
        ax = bits - 1 - b
        mine_bit = (me >> b) & 1
        keep = lax.dynamic_index_in_dim(cur, mine_bit, ax, keepdims=False)
        give = lax.dynamic_index_in_dim(cur, 1 - mine_bit, ax, keepdims=False)
        cur = keep + lax.ppermute(give, axis, [(i, i ^ (1 << b)) for i in range(n)])
    return cur


def doubling_gather(piece, axis, n, me):
    bits = n.bit_length() - 1
    cur = piece
    for b in range(bits):
        got = lax.ppermute(cur, axis, [(i, i ^ (1 << b)) for i in range(n)])
        low = ((me >> b) & 1) == 0
        cur = jnp.where(low, jnp.stack([cur, got]), jnp.stack([got, cur]))
    return cur.reshape((n,) + piece.shape)


def on_device(resid, enc_w, enc_b, dec_w, target, norm_gain, wq, wk, wv, prompt_ids):
    n_chip = lax.axis_size(CHIP)
    n_core = lax.axis_size("core")
    n_src = lax.axis_size("src")
    core = lax.axis_index("core")
    chip = lax.axis_index(CHIP)
    src = lax.axis_index("src")
    width_pos = chip * n_core + core
    rows_all = resid.shape[1]
    width_local = resid.shape[2]
    width_all = width_local * n_chip * n_core
    feats_all = enc_w.shape[2]
    share = feats_all // (n_chip * n_core)
    other = 1 - core

    x = resid[0]
    we = enc_w[0].reshape(width_local, n_chip, n_core, share)
    we_mine = lax.dynamic_index_in_dim(we, core, 2, keepdims=False).reshape(width_local, n_chip * share)
    we_give = lax.dynamic_index_in_dim(we, other, 2, keepdims=False).reshape(width_local, n_chip * share)
    we_got = lax.ppermute(we_give, "core", SWAP)
    x_got = lax.ppermute(x, "core", SWAP)
    pre = lax.dot_general(we_mine, x, (((0,), (1,)), ((), ())), preferred_element_type=jnp.float32)
    pre = pre + lax.dot_general(we_got, x_got, (((0,), (1,)), ((), ())), preferred_element_type=jnp.float32)
    pre_share = lax.psum_scatter(pre, CHIP, scatter_dimension=0, tiled=True)
    bias = lax.dynamic_slice_in_dim(enc_b[0], width_pos * share, share, 0)
    feats_t = jnp.maximum(pre_share + bias[:, None], 0.0).astype(jnp.bfloat16)
    feats = lax.all_gather(feats_t, WIDTH, axis=0, tiled=True)
    mlp_layer = contract0(feats, dec_w[0])

    query_rows = rows_all // n_src
    row_start = src * query_rows
    mlp = exchange_sum(mlp_layer.reshape(n_src, query_rows, width_local), "src", n_src, src)
    mlp_out = mlp.astype(jnp.bfloat16)
    tgt = lax.dynamic_slice_in_dim(target, row_start, query_rows, 0)
    stream = tgt.astype(jnp.float32) + mlp
    packed = jnp.concatenate([stream, norm_gain[None, :]], axis=0)
    packed_full = lax.all_gather(packed, WIDTH, axis=1, tiled=True)
    stream_full = packed_full[:query_rows]
    gain_full = packed_full[query_rows]
    power = jnp.sum(stream_full * stream_full, axis=1) / width_all
    scale = lax.rsqrt(power + 1e-05)[:, None]
    normed_full = (stream_full * scale * gain_full[None, :]).astype(jnp.bfloat16)
    normed_loc = (stream * scale * norm_gain[None, :]).astype(jnp.bfloat16)

    query = jnp.dot(normed_full, wq, preferred_element_type=jnp.float32).astype(jnp.bfloat16)
    n_kv = wk.shape[1] // HD
    key_part = jnp.dot(normed_loc, wk, preferred_element_type=jnp.float32).reshape(query_rows, n_kv, 1, HD)
    value_part = jnp.dot(normed_loc, wv, preferred_element_type=jnp.float32).reshape(query_rows, n_kv, 1, HD)
    kv_part = jnp.concatenate([key_part, value_part], axis=2).reshape(query_rows, n_kv * 2 * HD)
    n_width = n_chip * n_core
    quarter = kv_part.shape[1] // n_width
    kv_blocks = kv_part.reshape(query_rows, n_width, quarter).transpose(1, 0, 2)
    kv_share = halving_sum(kv_blocks, WIDTH, n_width, width_pos).astype(jnp.bfloat16)
    team = ("src", "wcl", "core")
    kv_all = doubling_gather(kv_share, team, n_src * 4, src * 4 + lax.axis_index("wcl") * 2 + core)
    kv_all = kv_all.reshape(n_src, -1, query_rows, quarter).transpose(0, 2, 1, 3).reshape(rows_all, -1)
    key_head = kv_all[:, :HD]
    value_head = kv_all[:, HD:]
    heads_here = wq.shape[1] // HD

    query3 = query.reshape(query_rows, heads_here, HD)
    scores = jnp.einsum(
        "qhd,sd->hqs", query3, key_head, preferred_element_type=jnp.float32
    ) / math.sqrt(HD)
    query_index = row_start + jnp.arange(query_rows, dtype=jnp.int32)
    key_index = jnp.arange(rows_all, dtype=jnp.int32)
    query_prompt = lax.dynamic_slice_in_dim(prompt_ids, row_start, query_rows, 0)
    allowed = (query_prompt[:, None] == prompt_ids[None, :]) & (
        key_index[None, :] <= query_index[:, None]
    )
    scores = jnp.where(allowed[None], scores, -1e30)
    peak = jnp.max(scores, axis=-1, keepdims=True)
    weights = jnp.exp(scores - peak)
    probs = (weights / jnp.sum(weights, axis=-1, keepdims=True)).astype(jnp.bfloat16)
    context = jnp.einsum("hqs,sd->qhd", probs, value_head, preferred_element_type=jnp.float32)
    return (mlp_out, context.reshape(query_rows, heads_here * HD).astype(jnp.bfloat16))


def solution(mesh):
    n_src = mesh.shape["src"]
    n_width = mesh.shape["width"]
    fine = Mesh(mesh.devices.reshape(n_src, n_width // 4, 2, 2), ("src", "wch", "wcl", "core"))
    in_specs = (
        P("src", None, WIDTH),
        P("src", WIDTH, None),
        P("src", None),
        P("src", None, WIDTH),
        P(None, WIDTH),
        P(WIDTH),
        P(None, WIDTH),
        P(WIDTH, None),
        P(WIDTH, None),
        P(),
    )
    out_specs = (P("src", WIDTH), P("src", WIDTH))
    return jax.shard_map(
        on_device, mesh=fine, in_specs=in_specs, out_specs=out_specs, check_vma=False
    )
```

```python
import math

import jax
import jax.numpy as jnp
from jax import lax
from jax.sharding import Mesh
from jax.sharding import PartitionSpec as P

HD = 128
GROUP = 8
WIDTH = ("wch", "wcl", "core")
CHIP = ("wch", "wcl")
SWAP = [(0, 1), (1, 0)]


def contract0(a, b):
    return lax.dot_general(a, b, (((0,), (0,)), ((), ())), preferred_element_type=jnp.float32)


def exchange_sum(blocks, axis, n, me):
    total = lax.dynamic_index_in_dim(blocks, me, 0, keepdims=False)
    for shift in range(1, n):
        piece = lax.dynamic_index_in_dim(blocks, (me + shift) % n, 0, keepdims=False)
        total = total + lax.ppermute(piece, axis, [(i, (i + shift) % n) for i in range(n)])
    return total


def halving_sum(blocks, axis, n, me):
    bits = n.bit_length() - 1
    rest = blocks.shape[1:]
    cur = blocks.reshape((2,) * bits + rest)
    for b in range(bits):
        ax = bits - 1 - b
        mine_bit = (me >> b) & 1
        keep = lax.dynamic_index_in_dim(cur, mine_bit, ax, keepdims=False)
        give = lax.dynamic_index_in_dim(cur, 1 - mine_bit, ax, keepdims=False)
        cur = keep + lax.ppermute(give, axis, [(i, i ^ (1 << b)) for i in range(n)])
    return cur


def doubling_gather(piece, axis, n, me):
    bits = n.bit_length() - 1
    cur = piece
    for b in range(bits):
        got = lax.ppermute(cur, axis, [(i, i ^ (1 << b)) for i in range(n)])
        low = ((me >> b) & 1) == 0
        cur = jnp.where(low, jnp.stack([cur, got]), jnp.stack([got, cur]))
    return cur.reshape((n,) + piece.shape)


def bit_reverse(x, bits):
    return sum(((x >> i) & 1) << (bits - 1 - i) for i in range(bits))


def halving_into(x, axis, n, pos, flips, dim):
    bits = n.bit_length() - 1
    size = x.shape[dim] // n
    cur = x
    for k in range(bits - 1, -1, -1):
        half = size << k
        b = (pos >> k) & 1
        keep = lax.dynamic_slice_in_dim(cur, b * half, half, dim)
        give = lax.dynamic_slice_in_dim(cur, (1 - b) * half, half, dim)
        pairs = [(i, i ^ (1 << flips[k])) for i in range(n)]
        cur = keep + lax.ppermute(give, axis, pairs)
    return cur


def doubling_into(piece, axis, n, pos, flips, dim):
    bits = n.bit_length() - 1
    size = piece.shape[dim]
    shape = list(piece.shape)
    shape[dim] = size * n
    buf = lax.dynamic_update_slice_in_dim(jnp.zeros(shape, piece.dtype), piece, pos * size, dim)
    for k in range(bits):
        base = (pos >> k) << k
        mine = lax.dynamic_slice_in_dim(buf, base * size, size << k, dim)
        pairs = [(i, i ^ (1 << flips[k])) for i in range(n)]
        got = lax.ppermute(mine, axis, pairs)
        buf = lax.dynamic_update_slice_in_dim(buf, got, (base ^ (1 << k)) * size, dim)
    return buf


def on_device(resid, enc_w, enc_b, dec_w, target, norm_gain, wq, wk, wv, prompt_ids):
    n_chip = lax.axis_size(CHIP)
    n_core = lax.axis_size("core")
    n_src = lax.axis_size("src")
    core = lax.axis_index("core")
    chip = lax.axis_index(CHIP)
    src = lax.axis_index("src")
    width_pos = chip * n_core + core
    rows_all = resid.shape[1]
    width_local = resid.shape[2]
    width_all = width_local * n_chip * n_core
    feats_all = enc_w.shape[2]
    share = feats_all // (n_chip * n_core)
    other = 1 - core

    n_width = n_chip * n_core
    w_bits = n_width.bit_length() - 1
    c_bits = n_chip.bit_length() - 1
    half = feats_all // n_core
    x = resid[0]
    we = enc_w[0]
    we_mine = lax.dynamic_slice_in_dim(we, core * half, half, 1)
    we_give = lax.dynamic_slice_in_dim(we, other * half, half, 1)
    we_got = lax.ppermute(we_give, "core", SWAP)
    x_got = lax.ppermute(x, "core", SWAP)
    pre = jnp.dot(x, we_mine, preferred_element_type=jnp.float32)
    pre = pre + jnp.dot(x_got, we_got, preferred_element_type=jnp.float32)
    chip_pos = bit_reverse(chip, c_bits)
    pre_share = halving_into(pre, CHIP, n_chip, chip_pos, [c_bits - 1 - k for k in range(c_bits)], 1)
    feat_pos = bit_reverse(width_pos, w_bits)
    bias = lax.dynamic_slice_in_dim(enc_b[0], feat_pos * share, share, 0)
    feats_t = jnp.maximum(pre_share + bias[None, :], 0.0).astype(jnp.bfloat16)
    feats = doubling_into(feats_t, WIDTH, n_width, feat_pos, [w_bits - 1 - k for k in range(w_bits)], 1)
    mlp_layer = jnp.dot(feats, dec_w[0], preferred_element_type=jnp.float32)

    query_rows = rows_all // n_src
    row_start = src * query_rows
    mlp = exchange_sum(mlp_layer.reshape(n_src, query_rows, width_local), "src", n_src, src)
    mlp_out = mlp.astype(jnp.bfloat16)
    tgt = lax.dynamic_slice_in_dim(target, row_start, query_rows, 0)
    stream = tgt.astype(jnp.float32) + mlp
    packed = jnp.concatenate([stream, norm_gain[None, :]], axis=0)
    packed_full = doubling_into(packed, WIDTH, n_width, width_pos, list(range(w_bits)), 1)
    stream_full = packed_full[:query_rows]
    gain_full = packed_full[query_rows]
    power = jnp.sum(stream_full * stream_full, axis=1) / width_all
    scale = lax.rsqrt(power + 1e-05)[:, None]
    normed_full = (stream_full * scale * gain_full[None, :]).astype(jnp.bfloat16)
    normed_loc = (stream * scale * norm_gain[None, :]).astype(jnp.bfloat16)

    query = jnp.dot(normed_full, wq, preferred_element_type=jnp.float32).astype(jnp.bfloat16)
    n_kv = wk.shape[1] // HD
    key_part = jnp.dot(normed_loc, wk, preferred_element_type=jnp.float32).reshape(query_rows, n_kv, 1, HD)
    value_part = jnp.dot(normed_loc, wv, preferred_element_type=jnp.float32).reshape(query_rows, n_kv, 1, HD)
    kv_part = jnp.concatenate([key_part, value_part], axis=2).reshape(query_rows, n_kv * 2 * HD)
    quarter = kv_part.shape[1] // n_width
    kv_blocks = kv_part.reshape(query_rows, n_width, quarter).transpose(1, 0, 2)
    kv_share = halving_sum(kv_blocks, WIDTH, n_width, width_pos).astype(jnp.bfloat16)
    team = ("src", "wcl", "core")
    kv_all = doubling_gather(kv_share, team, n_src * 4, src * 4 + lax.axis_index("wcl") * 2 + core)
    kv_all = kv_all.reshape(n_src, -1, query_rows, quarter).transpose(0, 2, 1, 3).reshape(rows_all, -1)
    key_head = kv_all[:, :HD]
    value_head = kv_all[:, HD:]
    heads_here = wq.shape[1] // HD

    query3 = query.reshape(query_rows, heads_here, HD)
    scores = jnp.einsum(
        "qhd,sd->hqs", query3, key_head, preferred_element_type=jnp.float32
    ) / math.sqrt(HD)
    query_index = row_start + jnp.arange(query_rows, dtype=jnp.int32)
    key_index = jnp.arange(rows_all, dtype=jnp.int32)
    query_prompt = lax.dynamic_slice_in_dim(prompt_ids, row_start, query_rows, 0)
    allowed = (query_prompt[:, None] == prompt_ids[None, :]) & (
        key_index[None, :] <= query_index[:, None]
    )
    scores = jnp.where(allowed[None], scores, -1e30)
    peak = jnp.max(scores, axis=-1, keepdims=True)
    weights = jnp.exp(scores - peak)
    probs = (weights / jnp.sum(weights, axis=-1, keepdims=True)).astype(jnp.bfloat16)
    context = jnp.einsum("hqs,sd->qhd", probs, value_head, preferred_element_type=jnp.float32)
    return (mlp_out, context.reshape(query_rows, heads_here * HD).astype(jnp.bfloat16))


def solution(mesh):
    n_src = mesh.shape["src"]
    n_width = mesh.shape["width"]
    fine = Mesh(mesh.devices.reshape(n_src, n_width // 4, 2, 2), ("src", "wch", "wcl", "core"))
    in_specs = (
        P("src", None, WIDTH),
        P("src", WIDTH, None),
        P("src", None),
        P("src", None, WIDTH),
        P(None, WIDTH),
        P(WIDTH),
        P(None, WIDTH),
        P(WIDTH, None),
        P(WIDTH, None),
        P(),
    )
    out_specs = (P("src", WIDTH), P("src", WIDTH))
    return jax.shard_map(
        on_device, mesh=fine, in_specs=in_specs, out_specs=out_specs, check_vma=False
    )
```

```python
import math

import jax
import jax.numpy as jnp
from jax import lax
from jax.sharding import Mesh
from jax.sharding import PartitionSpec as P

HD = 128
GROUP = 8
WIDTH = ("wch", "wcl", "core")
CHIP = ("wch", "wcl")
SWAP = [(0, 1), (1, 0)]


def contract0(a, b):
    return lax.dot_general(a, b, (((0,), (0,)), ((), ())), preferred_element_type=jnp.float32)


def exchange_sum(blocks, axis, n, me):
    total = lax.dynamic_index_in_dim(blocks, me, 0, keepdims=False)
    for shift in range(1, n):
        piece = lax.dynamic_index_in_dim(blocks, (me + shift) % n, 0, keepdims=False)
        total = total + lax.ppermute(piece, axis, [(i, (i + shift) % n) for i in range(n)])
    return total


def halving_sum(blocks, axis, n, me):
    bits = n.bit_length() - 1
    rest = blocks.shape[1:]
    cur = blocks.reshape((2,) * bits + rest)
    for b in range(bits):
        ax = bits - 1 - b
        mine_bit = (me >> b) & 1
        keep = lax.dynamic_index_in_dim(cur, mine_bit, ax, keepdims=False)
        give = lax.dynamic_index_in_dim(cur, 1 - mine_bit, ax, keepdims=False)
        cur = keep + lax.ppermute(give, axis, [(i, i ^ (1 << b)) for i in range(n)])
    return cur


def doubling_gather(piece, axis, n, me):
    bits = n.bit_length() - 1
    cur = piece
    for b in range(bits):
        got = lax.ppermute(cur, axis, [(i, i ^ (1 << b)) for i in range(n)])
        low = ((me >> b) & 1) == 0
        cur = jnp.where(low, jnp.stack([cur, got]), jnp.stack([got, cur]))
    return cur.reshape((n,) + piece.shape)


def on_device(resid, enc_w, enc_b, dec_w, target, norm_gain, wq, wk, wv, prompt_ids):
    n_chip = lax.axis_size(CHIP)
    n_core = lax.axis_size("core")
    n_src = lax.axis_size("src")
    core = lax.axis_index("core")
    chip = lax.axis_index(CHIP)
    src = lax.axis_index("src")
    width_pos = chip * n_core + core
    rows_all = resid.shape[1]
    width_local = resid.shape[2]
    width_all = width_local * n_chip * n_core
    feats_all = enc_w.shape[2]
    share = feats_all // (n_chip * n_core)
    other = 1 - core

    x = resid[0]
    we = enc_w[0].reshape(width_local, n_chip, n_core, share)
    we_mine = lax.dynamic_index_in_dim(we, core, 2, keepdims=False).reshape(width_local, n_chip * share)
    we_give = lax.dynamic_index_in_dim(we, other, 2, keepdims=False).reshape(width_local, n_chip * share)
    we_got = lax.ppermute(we_give, "core", SWAP)
    x_got = lax.ppermute(x, "core", SWAP)
    pre = lax.dot_general(we_mine, x, (((0,), (1,)), ((), ())), preferred_element_type=jnp.float32)
    pre = pre + lax.dot_general(we_got, x_got, (((0,), (1,)), ((), ())), preferred_element_type=jnp.float32)
    pre_share = lax.psum_scatter(pre, CHIP, scatter_dimension=0, tiled=True)
    bias = lax.dynamic_slice_in_dim(enc_b[0], width_pos * share, share, 0)
    feats_t = jnp.maximum(pre_share + bias[:, None], 0.0).astype(jnp.bfloat16)
    feats = lax.all_gather(feats_t, WIDTH, axis=0, tiled=True)
    mlp_cols = contract0(dec_w[0], feats)

    query_rows = rows_all // n_src
    row_start = src * query_rows
    mlp_blocks = mlp_cols.reshape(width_local, n_src, query_rows).transpose(1, 0, 2)
    mlp = exchange_sum(mlp_blocks, "src", n_src, src).T
    mlp_out = mlp.astype(jnp.bfloat16)
    tgt = lax.dynamic_slice_in_dim(target, row_start, query_rows, 0)
    stream = tgt.astype(jnp.float32) + mlp
    n_width = n_chip * n_core
    n_kv = wk.shape[1] // HD
    lifted = stream * norm_gain[None, :]
    exact = lax.Precision.HIGHEST
    key_part = jnp.dot(lifted, wk.astype(jnp.float32), precision=exact).reshape(query_rows, n_kv, 1, HD)
    value_part = jnp.dot(lifted, wv.astype(jnp.float32), precision=exact).reshape(query_rows, n_kv, 1, HD)
    kv_part = jnp.concatenate([key_part, value_part], axis=2).reshape(query_rows, n_kv * 2 * HD)
    quarter = kv_part.shape[1] // n_width
    kv_blocks = kv_part.reshape(query_rows, n_width, quarter).transpose(1, 0, 2)
    kv_sum = halving_sum(kv_blocks, WIDTH, n_width, width_pos)

    packed = jnp.concatenate([stream, norm_gain[None, :]], axis=0)
    packed_full = lax.all_gather(packed, WIDTH, axis=1, tiled=True)
    stream_full = packed_full[:query_rows]
    gain_full = packed_full[query_rows]
    power = jnp.sum(stream_full * stream_full, axis=1) / width_all
    scale = lax.rsqrt(power + 1e-05)[:, None]
    normed_full = (stream_full * scale * gain_full[None, :]).astype(jnp.bfloat16)
    query = jnp.dot(normed_full, wq, preferred_element_type=jnp.float32).astype(jnp.bfloat16)

    kv_share = (kv_sum * scale).astype(jnp.bfloat16)
    team = ("src", "wcl", "core")
    kv_all = doubling_gather(kv_share, team, n_src * 4, src * 4 + lax.axis_index("wcl") * 2 + core)
    kv_all = kv_all.reshape(n_src, -1, query_rows, quarter).transpose(0, 2, 1, 3).reshape(rows_all, -1)
    key_head = kv_all[:, :HD]
    value_head = kv_all[:, HD:]
    heads_here = wq.shape[1] // HD

    query3 = query.reshape(query_rows, heads_here, HD)
    scores = jnp.einsum(
        "qhd,sd->hqs", query3, key_head, preferred_element_type=jnp.float32
    ) / math.sqrt(HD)
    query_index = row_start + jnp.arange(query_rows, dtype=jnp.int32)
    key_index = jnp.arange(rows_all, dtype=jnp.int32)
    query_prompt = lax.dynamic_slice_in_dim(prompt_ids, row_start, query_rows, 0)
    allowed = (query_prompt[:, None] == prompt_ids[None, :]) & (
        key_index[None, :] <= query_index[:, None]
    )
    scores = jnp.where(allowed[None], scores, -1e30)
    peak = jnp.max(scores, axis=-1, keepdims=True)
    weights = jnp.exp(scores - peak)
    probs = (weights / jnp.sum(weights, axis=-1, keepdims=True)).astype(jnp.bfloat16)
    context = jnp.einsum("hqs,sd->qhd", probs, value_head, preferred_element_type=jnp.float32)
    return (mlp_out, context.reshape(query_rows, heads_here * HD).astype(jnp.bfloat16))


def solution(mesh):
    n_src = mesh.shape["src"]
    n_width = mesh.shape["width"]
    fine = Mesh(mesh.devices.reshape(n_src, n_width // 4, 2, 2), ("src", "wch", "wcl", "core"))
    in_specs = (
        P("src", None, WIDTH),
        P("src", WIDTH, None),
        P("src", None),
        P("src", None, WIDTH),
        P(None, WIDTH),
        P(WIDTH),
        P(None, WIDTH),
        P(WIDTH, None),
        P(WIDTH, None),
        P(),
    )
    out_specs = (P("src", WIDTH), P("src", WIDTH))
    return jax.shard_map(
        on_device, mesh=fine, in_specs=in_specs, out_specs=out_specs, check_vma=False
    )
```

```python
import math

import jax
import jax.numpy as jnp
from jax import lax
from jax.sharding import Mesh
from jax.sharding import PartitionSpec as P

HD = 128
GROUP = 8
WIDTH = ("wch", "wcl", "core")
CHIP = ("wch", "wcl")
SWAP = [(0, 1), (1, 0)]


def contract0(a, b):
    return lax.dot_general(a, b, (((0,), (0,)), ((), ())), preferred_element_type=jnp.float32)


def exchange_sum(blocks, axis, n, me):
    total = lax.dynamic_index_in_dim(blocks, me, 0, keepdims=False)
    for shift in range(1, n):
        piece = lax.dynamic_index_in_dim(blocks, (me + shift) % n, 0, keepdims=False)
        total = total + lax.ppermute(piece, axis, [(i, (i + shift) % n) for i in range(n)])
    return total


def halving_sum(blocks, axis, n, me):
    bits = n.bit_length() - 1
    rest = blocks.shape[1:]
    cur = blocks.reshape((2,) * bits + rest)
    for b in range(bits):
        ax = bits - 1 - b
        mine_bit = (me >> b) & 1
        keep = lax.dynamic_index_in_dim(cur, mine_bit, ax, keepdims=False)
        give = lax.dynamic_index_in_dim(cur, 1 - mine_bit, ax, keepdims=False)
        cur = keep + lax.ppermute(give, axis, [(i, i ^ (1 << b)) for i in range(n)])
    return cur


def doubling_gather(piece, axis, n, me):
    bits = n.bit_length() - 1
    cur = piece
    for b in range(bits):
        got = lax.ppermute(cur, axis, [(i, i ^ (1 << b)) for i in range(n)])
        low = ((me >> b) & 1) == 0
        cur = jnp.where(low, jnp.stack([cur, got]), jnp.stack([got, cur]))
    return cur.reshape((n,) + piece.shape)


def on_device(resid, enc_w, enc_b, dec_w, target, norm_gain, wq, wk, wv, prompt_ids):
    n_chip = lax.axis_size(CHIP)
    n_core = lax.axis_size("core")
    n_src = lax.axis_size("src")
    core = lax.axis_index("core")
    chip = lax.axis_index(CHIP)
    src = lax.axis_index("src")
    width_pos = chip * n_core + core
    rows_all = resid.shape[1]
    width_local = resid.shape[2]
    width_all = width_local * n_chip * n_core
    feats_all = enc_w.shape[2]
    share = feats_all // (n_chip * n_core)
    other = 1 - core

    x = resid[0]
    we = enc_w[0].reshape(width_local, n_chip, n_core, share)
    we_mine = lax.dynamic_index_in_dim(we, core, 2, keepdims=False).reshape(width_local, n_chip * share)
    we_give = lax.dynamic_index_in_dim(we, other, 2, keepdims=False).reshape(width_local, n_chip * share)
    we_got = lax.ppermute(we_give, "core", SWAP)
    x_got = lax.ppermute(x, "core", SWAP)
    pre = lax.dot_general(we_mine, x, (((0,), (1,)), ((), ())), preferred_element_type=jnp.float32)
    pre = pre + lax.dot_general(we_got, x_got, (((0,), (1,)), ((), ())), preferred_element_type=jnp.float32)
    pre_share = lax.psum_scatter(pre, CHIP, scatter_dimension=0, tiled=True)
    bias = lax.dynamic_slice_in_dim(enc_b[0], width_pos * share, share, 0)
    feats_t = jnp.maximum(pre_share + bias[:, None], 0.0).astype(jnp.bfloat16)
    feats = lax.all_gather(feats_t, WIDTH, axis=0, tiled=True)
    mlp_cols = contract0(dec_w[0], feats)

    query_rows = rows_all // n_src
    row_start = src * query_rows
    mlp_blocks = mlp_cols.reshape(width_local, n_src, query_rows).transpose(1, 0, 2)
    mlp = exchange_sum(mlp_blocks, "src", n_src, src).T
    mlp_out = mlp.astype(jnp.bfloat16)
    tgt = lax.dynamic_slice_in_dim(target, row_start, query_rows, 0)
    stream = tgt.astype(jnp.float32) + mlp
    n_width = n_chip * n_core
    n_kv = wk.shape[1] // HD
    lifted = stream * norm_gain[None, :]
    exact = lax.Precision.HIGHEST
    key_part = jnp.dot(lifted, wk.astype(jnp.float32), precision=exact).reshape(query_rows, n_kv, 1, HD)
    value_part = jnp.dot(lifted, wv.astype(jnp.float32), precision=exact).reshape(query_rows, n_kv, 1, HD)
    kv_part = jnp.concatenate([key_part, value_part], axis=2).reshape(query_rows, n_kv * 2 * HD)
    quarter = kv_part.shape[1] // n_width
    kv_blocks = kv_part.reshape(query_rows, n_width, quarter).transpose(1, 0, 2)
    row_power = jnp.sum(stream * stream, axis=1)
    power_col = jnp.broadcast_to(row_power[None, :, None], (n_width, query_rows, 1))
    kv_sum = halving_sum(jnp.concatenate([kv_blocks, power_col], axis=2), WIDTH, n_width, width_pos)
    kv_scale = lax.rsqrt(kv_sum[:, quarter] / width_all + 1e-05)[:, None]
    kv_share = (kv_sum[:, :quarter] * kv_scale).astype(jnp.bfloat16)
    team = ("src", "wcl", "core")
    kv_all = doubling_gather(kv_share, team, n_src * 4, src * 4 + lax.axis_index("wcl") * 2 + core)

    packed = jnp.concatenate([stream, norm_gain[None, :]], axis=0)
    packed_full = lax.all_gather(packed, WIDTH, axis=1, tiled=True)
    stream_full = packed_full[:query_rows]
    gain_full = packed_full[query_rows]
    power = jnp.sum(stream_full * stream_full, axis=1) / width_all
    scale = lax.rsqrt(power + 1e-05)[:, None]
    normed_full = (stream_full * scale * gain_full[None, :]).astype(jnp.bfloat16)
    query = jnp.dot(normed_full, wq, preferred_element_type=jnp.float32).astype(jnp.bfloat16)

    kv_all = kv_all.reshape(n_src, -1, query_rows, quarter).transpose(0, 2, 1, 3).reshape(rows_all, -1)
    key_head = kv_all[:, :HD]
    value_head = kv_all[:, HD:]
    heads_here = wq.shape[1] // HD

    query3 = query.reshape(query_rows, heads_here, HD)
    scores = jnp.einsum(
        "qhd,sd->hqs", query3, key_head, preferred_element_type=jnp.float32
    ) / math.sqrt(HD)
    query_index = row_start + jnp.arange(query_rows, dtype=jnp.int32)
    key_index = jnp.arange(rows_all, dtype=jnp.int32)
    query_prompt = lax.dynamic_slice_in_dim(prompt_ids, row_start, query_rows, 0)
    allowed = (query_prompt[:, None] == prompt_ids[None, :]) & (
        key_index[None, :] <= query_index[:, None]
    )
    scores = jnp.where(allowed[None], scores, -1e30)
    peak = jnp.max(scores, axis=-1, keepdims=True)
    weights = jnp.exp(scores - peak)
    probs = (weights / jnp.sum(weights, axis=-1, keepdims=True)).astype(jnp.bfloat16)
    context = jnp.einsum("hqs,sd->qhd", probs, value_head, preferred_element_type=jnp.float32)
    return (mlp_out, context.reshape(query_rows, heads_here * HD).astype(jnp.bfloat16))


def solution(mesh):
    n_src = mesh.shape["src"]
    n_width = mesh.shape["width"]
    fine = Mesh(mesh.devices.reshape(n_src, n_width // 4, 2, 2), ("src", "wch", "wcl", "core"))
    in_specs = (
        P("src", None, WIDTH),
        P("src", WIDTH, None),
        P("src", None),
        P("src", None, WIDTH),
        P(None, WIDTH),
        P(WIDTH),
        P(None, WIDTH),
        P(WIDTH, None),
        P(WIDTH, None),
        P(),
    )
    out_specs = (P("src", WIDTH), P("src", WIDTH))
    return jax.shard_map(
        on_device, mesh=fine, in_specs=in_specs, out_specs=out_specs, check_vma=False
    )
```

```python
import math

import jax
import jax.numpy as jnp
from jax import lax
from jax.sharding import Mesh
from jax.sharding import PartitionSpec as P

HD = 128
GROUP = 8
WIDTH = ("wch", "wcl", "core")
CHIP = ("wch", "wcl")
SWAP = [(0, 1), (1, 0)]


def contract0(a, b):
    return lax.dot_general(a, b, (((0,), (0,)), ((), ())), preferred_element_type=jnp.float32)


def exchange_sum(blocks, axis, n, me):
    total = lax.dynamic_index_in_dim(blocks, me, 0, keepdims=False)
    for shift in range(1, n):
        piece = lax.dynamic_index_in_dim(blocks, (me + shift) % n, 0, keepdims=False)
        total = total + lax.ppermute(piece, axis, [(i, (i + shift) % n) for i in range(n)])
    return total


def halving_sum(blocks, axis, n, me):
    bits = n.bit_length() - 1
    rest = blocks.shape[1:]
    cur = blocks.reshape((2,) * bits + rest)
    for b in range(bits):
        ax = bits - 1 - b
        mine_bit = (me >> b) & 1
        keep = lax.dynamic_index_in_dim(cur, mine_bit, ax, keepdims=False)
        give = lax.dynamic_index_in_dim(cur, 1 - mine_bit, ax, keepdims=False)
        cur = keep + lax.ppermute(give, axis, [(i, i ^ (1 << b)) for i in range(n)])
    return cur


def doubling_gather(piece, axis, n, me):
    bits = n.bit_length() - 1
    cur = piece
    for b in range(bits):
        got = lax.ppermute(cur, axis, [(i, i ^ (1 << b)) for i in range(n)])
        low = ((me >> b) & 1) == 0
        cur = jnp.where(low, jnp.stack([cur, got]), jnp.stack([got, cur]))
    return cur.reshape((n,) + piece.shape)


def on_device(resid, enc_w, enc_b, dec_w, target, norm_gain, wq, wk, wv, prompt_ids):
    n_chip = lax.axis_size(CHIP)
    n_core = lax.axis_size("core")
    n_src = lax.axis_size("src")
    core = lax.axis_index("core")
    chip = lax.axis_index(CHIP)
    src = lax.axis_index("src")
    width_pos = chip * n_core + core
    rows_all = resid.shape[1]
    width_local = resid.shape[2]
    width_all = width_local * n_chip * n_core
    feats_all = enc_w.shape[2]
    share = feats_all // (n_chip * n_core)
    other = 1 - core

    x = resid[0]
    we = enc_w[0].reshape(width_local, n_chip, n_core, share)
    we_mine = lax.dynamic_index_in_dim(we, core, 2, keepdims=False).reshape(width_local, n_chip * share)
    we_give = lax.dynamic_index_in_dim(we, other, 2, keepdims=False).reshape(width_local, n_chip * share)
    we_got = lax.ppermute(we_give, "core", SWAP)
    x_got = lax.ppermute(x, "core", SWAP)
    pre = lax.dot_general(we_mine, x, (((0,), (1,)), ((), ())), preferred_element_type=jnp.float32)
    pre = pre + lax.dot_general(we_got, x_got, (((0,), (1,)), ((), ())), preferred_element_type=jnp.float32)
    pre_share = lax.psum_scatter(pre.astype(jnp.bfloat16), CHIP, scatter_dimension=0, tiled=True)
    bias = lax.dynamic_slice_in_dim(enc_b[0], width_pos * share, share, 0)
    feats_t = jnp.maximum(pre_share.astype(jnp.float32) + bias[:, None], 0.0).astype(jnp.bfloat16)
    feats = lax.all_gather(feats_t, WIDTH, axis=0, tiled=True)
    mlp_cols = contract0(dec_w[0], feats)

    query_rows = rows_all // n_src
    row_start = src * query_rows
    mlp_blocks = mlp_cols.reshape(width_local, n_src, query_rows).transpose(1, 0, 2)
    mlp = halving_sum(mlp_blocks, "src", n_src, src).T
    mlp_out = mlp.astype(jnp.bfloat16)
    tgt = lax.dynamic_slice_in_dim(target, row_start, query_rows, 0)
    stream = tgt.astype(jnp.float32) + mlp
    n_width = n_chip * n_core
    n_kv = wk.shape[1] // HD
    lifted = stream * norm_gain[None, :]
    exact = lax.Precision.HIGHEST
    key_part = jnp.dot(lifted, wk.astype(jnp.float32), precision=exact).reshape(query_rows, n_kv, 1, HD)
    value_part = jnp.dot(lifted, wv.astype(jnp.float32), precision=exact).reshape(query_rows, n_kv, 1, HD)
    kv_part = jnp.concatenate([key_part, value_part], axis=2).reshape(query_rows, n_kv * 2 * HD)
    quarter = kv_part.shape[1] // n_width
    kv_blocks = kv_part.reshape(query_rows, n_width, quarter).transpose(1, 0, 2)
    row_power = jnp.sum(stream * stream, axis=1)
    power_col = jnp.broadcast_to(row_power[None, :, None], (n_width, query_rows, 1))
    kv_sum = halving_sum(jnp.concatenate([kv_blocks, power_col], axis=2), WIDTH, n_width, width_pos)
    kv_scale = lax.rsqrt(kv_sum[:, quarter] / width_all + 1e-05)[:, None]
    kv_share = (kv_sum[:, :quarter] * kv_scale).astype(jnp.bfloat16)
    team = ("src", "wcl", "core")
    kv_all = doubling_gather(kv_share, team, n_src * 4, src * 4 + lax.axis_index("wcl") * 2 + core)

    packed = jnp.concatenate([stream, norm_gain[None, :]], axis=0)
    packed_full = lax.all_gather(packed, WIDTH, axis=1, tiled=True)
    stream_full = packed_full[:query_rows]
    gain_full = packed_full[query_rows]
    power = jnp.sum(stream_full * stream_full, axis=1) / width_all
    scale = lax.rsqrt(power + 1e-05)[:, None]
    normed_full = (stream_full * scale * gain_full[None, :]).astype(jnp.bfloat16)
    query = jnp.dot(normed_full, wq, preferred_element_type=jnp.float32).astype(jnp.bfloat16)

    kv_all = kv_all.reshape(n_src, -1, query_rows, quarter).transpose(0, 2, 1, 3).reshape(rows_all, -1)
    key_head = kv_all[:, :HD]
    value_head = kv_all[:, HD:]
    heads_here = wq.shape[1] // HD

    query3 = query.reshape(query_rows, heads_here, HD)
    scores = jnp.einsum(
        "qhd,sd->hqs", query3, key_head, preferred_element_type=jnp.float32
    ) / math.sqrt(HD)
    query_index = row_start + jnp.arange(query_rows, dtype=jnp.int32)
    key_index = jnp.arange(rows_all, dtype=jnp.int32)
    query_prompt = lax.dynamic_slice_in_dim(prompt_ids, row_start, query_rows, 0)
    allowed = (query_prompt[:, None] == prompt_ids[None, :]) & (
        key_index[None, :] <= query_index[:, None]
    )
    scores = jnp.where(allowed[None], scores, -1e30)
    peak = jnp.max(scores, axis=-1, keepdims=True)
    weights = jnp.exp(scores - peak)
    probs = (weights / jnp.sum(weights, axis=-1, keepdims=True)).astype(jnp.bfloat16)
    context = jnp.einsum("hqs,sd->qhd", probs, value_head, preferred_element_type=jnp.float32)
    return (mlp_out, context.reshape(query_rows, heads_here * HD).astype(jnp.bfloat16))


def solution(mesh):
    n_src = mesh.shape["src"]
    n_width = mesh.shape["width"]
    fine = Mesh(mesh.devices.reshape(n_src, n_width // 4, 2, 2), ("src", "wch", "wcl", "core"))
    in_specs = (
        P("src", None, WIDTH),
        P("src", WIDTH, None),
        P("src", None),
        P("src", None, WIDTH),
        P(None, WIDTH),
        P(WIDTH),
        P(None, WIDTH),
        P(WIDTH, None),
        P(WIDTH, None),
        P(),
    )
    out_specs = (P("src", WIDTH), P("src", WIDTH))
    return jax.shard_map(
        on_device, mesh=fine, in_specs=in_specs, out_specs=out_specs, check_vma=False
    )
```

```python
import math

import jax
import jax.numpy as jnp
from jax import lax
from jax.sharding import Mesh
from jax.sharding import PartitionSpec as P

HD = 128
GROUP = 8
WIDTH = ("wch", "wcl", "core")
CHIP = ("wch", "wcl")
SWAP = [(0, 1), (1, 0)]


def contract0(a, b):
    return lax.dot_general(a, b, (((0,), (0,)), ((), ())), preferred_element_type=jnp.float32)


def exchange_sum(blocks, axis, n, me):
    total = lax.dynamic_index_in_dim(blocks, me, 0, keepdims=False)
    for shift in range(1, n):
        piece = lax.dynamic_index_in_dim(blocks, (me + shift) % n, 0, keepdims=False)
        total = total + lax.ppermute(piece, axis, [(i, (i + shift) % n) for i in range(n)])
    return total


def halving_sum(blocks, axis, n, me):
    bits = n.bit_length() - 1
    rest = blocks.shape[1:]
    cur = blocks.reshape((2,) * bits + rest)
    for b in range(bits):
        ax = bits - 1 - b
        mine_bit = (me >> b) & 1
        keep = lax.dynamic_index_in_dim(cur, mine_bit, ax, keepdims=False)
        give = lax.dynamic_index_in_dim(cur, 1 - mine_bit, ax, keepdims=False)
        cur = keep + lax.ppermute(give, axis, [(i, i ^ (1 << b)) for i in range(n)])
    return cur


def halving_bits(blocks, axis, n, me, flips):
    kbits = len(flips)
    rest = blocks.shape[1:]
    cur = blocks.reshape((2,) * kbits + rest)
    for k in range(kbits):
        ax = kbits - 1 - k
        mine_bit = (me >> flips[k]) & 1
        keep = lax.dynamic_index_in_dim(cur, mine_bit, ax, keepdims=False)
        give = lax.dynamic_index_in_dim(cur, 1 - mine_bit, ax, keepdims=False)
        cur = keep + lax.ppermute(give, axis, [(i, i ^ (1 << flips[k])) for i in range(n)])
    return cur


def doubling_gather(piece, axis, n, me):
    bits = n.bit_length() - 1
    cur = piece
    for b in range(bits):
        got = lax.ppermute(cur, axis, [(i, i ^ (1 << b)) for i in range(n)])
        low = ((me >> b) & 1) == 0
        cur = jnp.where(low, jnp.stack([cur, got]), jnp.stack([got, cur]))
    return cur.reshape((n,) + piece.shape)


def on_device(resid, enc_w, enc_b, dec_w, target, norm_gain, wq, wk, wv, prompt_ids):
    n_chip = lax.axis_size(CHIP)
    n_core = lax.axis_size("core")
    n_src = lax.axis_size("src")
    core = lax.axis_index("core")
    chip = lax.axis_index(CHIP)
    src = lax.axis_index("src")
    width_pos = chip * n_core + core
    rows_all = resid.shape[1]
    width_local = resid.shape[2]
    width_all = width_local * n_chip * n_core
    feats_all = enc_w.shape[2]
    share = feats_all // (n_chip * n_core)
    other = 1 - core

    half = feats_all // n_core
    x = resid[0]
    we = enc_w[0]
    we_mine = lax.dynamic_slice_in_dim(we, core * half, half, 1)
    we_give = lax.dynamic_slice_in_dim(we, other * half, half, 1)
    we_got = lax.ppermute(we_give, "core", SWAP)
    x_got = lax.ppermute(x, "core", SWAP)
    pre = lax.dot_general(we_mine, x, (((0,), (1,)), ((), ())), preferred_element_type=jnp.float32)
    pre = pre + lax.dot_general(we_got, x_got, (((0,), (1,)), ((), ())), preferred_element_type=jnp.float32)
    pre_share = lax.psum_scatter(pre, CHIP, scatter_dimension=0, tiled=True)
    bias = lax.dynamic_slice_in_dim(enc_b[0], (core * n_chip + chip) * share, share, 0)
    feats_t = jnp.maximum(pre_share + bias[:, None], 0.0).astype(jnp.bfloat16)
    feats = lax.all_gather(feats_t, WIDTH, axis=0, tiled=True)
    wd = dec_w[0].reshape(n_core, n_chip, share, width_local).transpose(1, 0, 2, 3)
    wd = wd.reshape(feats_all, width_local)
    mlp_cols = contract0(wd, feats)

    query_rows = rows_all // n_src
    row_start = src * query_rows
    mlp_blocks = mlp_cols.reshape(width_local, n_src, query_rows).transpose(1, 0, 2)
    mlp = halving_sum(mlp_blocks, "src", n_src, src).T
    mlp_out = mlp.astype(jnp.bfloat16)
    tgt = lax.dynamic_slice_in_dim(target, row_start, query_rows, 0)
    stream = tgt.astype(jnp.float32) + mlp
    n_width = n_chip * n_core
    n_kv = wk.shape[1] // HD
    lifted = stream * norm_gain[None, :]
    exact = lax.Precision.HIGHEST
    key_part = jnp.dot(lifted, wk.astype(jnp.float32), precision=exact).reshape(query_rows, n_kv, 1, HD)
    value_part = jnp.dot(lifted, wv.astype(jnp.float32), precision=exact).reshape(query_rows, n_kv, 1, HD)
    kv_part = jnp.concatenate([key_part, value_part], axis=2).reshape(query_rows, n_kv * 2 * HD)
    head_cols = 2 * HD
    n_heads_kv = kv_part.shape[1] // head_cols
    kv_blocks = kv_part.reshape(query_rows, n_heads_kv, head_cols).transpose(1, 0, 2)
    row_power = jnp.sum(stream * stream, axis=1)
    power_col = jnp.broadcast_to(row_power[None, :, None], (n_heads_kv, query_rows, 1))
    kv_blocks = jnp.concatenate([kv_blocks, power_col], axis=2)
    w_bits = n_width.bit_length() - 1
    low_bits = w_bits - (n_heads_kv.bit_length() - 1)
    kv_sum = halving_bits(kv_blocks, WIDTH, n_width, width_pos, list(range(low_bits, w_bits)))
    for b in range(low_bits):
        kv_sum = kv_sum + lax.ppermute(kv_sum, WIDTH, [(i, i ^ (1 << b)) for i in range(n_width)])
    kv_scale = lax.rsqrt(kv_sum[:, head_cols] / width_all + 1e-05)[:, None]
    kv_head = (kv_sum[:, :head_cols] * kv_scale).astype(jnp.bfloat16)
    kv_all = doubling_gather(kv_head, "src", n_src, src).reshape(rows_all, head_cols)

    packed = jnp.concatenate([stream, norm_gain[None, :]], axis=0)
    packed_full = lax.all_gather(packed, WIDTH, axis=1, tiled=True)
    stream_full = packed_full[:query_rows]
    gain_full = packed_full[query_rows]
    power = jnp.sum(stream_full * stream_full, axis=1) / width_all
    scale = lax.rsqrt(power + 1e-05)[:, None]
    normed_full = (stream_full * scale * gain_full[None, :]).astype(jnp.bfloat16)
    query = jnp.dot(normed_full, wq, preferred_element_type=jnp.float32).astype(jnp.bfloat16)

    key_head = kv_all[:, :HD]
    value_head = kv_all[:, HD:]
    heads_here = wq.shape[1] // HD

    query3 = query.reshape(query_rows, heads_here, HD)
    scores = jnp.einsum(
        "qhd,sd->hqs", query3, key_head, preferred_element_type=jnp.float32
    ) / math.sqrt(HD)
    query_index = row_start + jnp.arange(query_rows, dtype=jnp.int32)
    key_index = jnp.arange(rows_all, dtype=jnp.int32)
    query_prompt = lax.dynamic_slice_in_dim(prompt_ids, row_start, query_rows, 0)
    allowed = (query_prompt[:, None] == prompt_ids[None, :]) & (
        key_index[None, :] <= query_index[:, None]
    )
    scores = jnp.where(allowed[None], scores, -1e30)
    peak = jnp.max(scores, axis=-1, keepdims=True)
    weights = jnp.exp(scores - peak)
    probs = (weights / jnp.sum(weights, axis=-1, keepdims=True)).astype(jnp.bfloat16)
    context = jnp.einsum("hqs,sd->qhd", probs, value_head, preferred_element_type=jnp.float32)
    return (mlp_out, context.reshape(query_rows, heads_here * HD).astype(jnp.bfloat16))


def solution(mesh):
    n_src = mesh.shape["src"]
    n_width = mesh.shape["width"]
    fine = Mesh(mesh.devices.reshape(n_src, n_width // 4, 2, 2), ("src", "wch", "wcl", "core"))
    in_specs = (
        P("src", None, WIDTH),
        P("src", WIDTH, None),
        P("src", None),
        P("src", None, WIDTH),
        P(None, WIDTH),
        P(WIDTH),
        P(None, WIDTH),
        P(WIDTH, None),
        P(WIDTH, None),
        P(),
    )
    out_specs = (P("src", WIDTH), P("src", WIDTH))
    return jax.shard_map(
        on_device, mesh=fine, in_specs=in_specs, out_specs=out_specs, check_vma=False
    )
```

```python
import math

import jax
import jax.numpy as jnp
from jax import lax
from jax.sharding import Mesh
from jax.sharding import PartitionSpec as P

HD = 128
GROUP = 8
WIDTH = ("wz", "wx", "core")
CHIP = ("wz", "wx")
SWAP = [(0, 1), (1, 0)]


def contract0(a, b):
    return lax.dot_general(a, b, (((0,), (0,)), ((), ())), preferred_element_type=jnp.float32)


def exchange_sum(blocks, axis, n, me):
    total = lax.dynamic_index_in_dim(blocks, me, 0, keepdims=False)
    for shift in range(1, n):
        piece = lax.dynamic_index_in_dim(blocks, (me + shift) % n, 0, keepdims=False)
        total = total + lax.ppermute(piece, axis, [(i, (i + shift) % n) for i in range(n)])
    return total


def halving_sum(blocks, axis, n, me):
    bits = n.bit_length() - 1
    rest = blocks.shape[1:]
    cur = blocks.reshape((2,) * bits + rest)
    for b in range(bits):
        ax = bits - 1 - b
        mine_bit = (me >> b) & 1
        keep = lax.dynamic_index_in_dim(cur, mine_bit, ax, keepdims=False)
        give = lax.dynamic_index_in_dim(cur, 1 - mine_bit, ax, keepdims=False)
        cur = keep + lax.ppermute(give, axis, [(i, i ^ (1 << b)) for i in range(n)])
    return cur


def halving_bits(blocks, axis, n, me, flips):
    kbits = len(flips)
    rest = blocks.shape[1:]
    cur = blocks.reshape((2,) * kbits + rest)
    for k in range(kbits):
        ax = kbits - 1 - k
        mine_bit = (me >> flips[k]) & 1
        keep = lax.dynamic_index_in_dim(cur, mine_bit, ax, keepdims=False)
        give = lax.dynamic_index_in_dim(cur, 1 - mine_bit, ax, keepdims=False)
        cur = keep + lax.ppermute(give, axis, [(i, i ^ (1 << flips[k])) for i in range(n)])
    return cur


def doubling_gather(piece, axis, n, me):
    bits = n.bit_length() - 1
    cur = piece
    for b in range(bits):
        got = lax.ppermute(cur, axis, [(i, i ^ (1 << b)) for i in range(n)])
        low = ((me >> b) & 1) == 0
        cur = jnp.where(low, jnp.stack([cur, got]), jnp.stack([got, cur]))
    return cur.reshape((n,) + piece.shape)


def on_device(resid, enc_w, enc_b, dec_w, target, norm_gain, wq, wk, wv, prompt_ids):
    n_chip = lax.axis_size(CHIP)
    n_core = lax.axis_size("core")
    n_src = lax.axis_size("src")
    core = lax.axis_index("core")
    chip = lax.axis_index(CHIP)
    src = lax.axis_index("src")
    width_pos = chip * n_core + core
    rows_all = resid.shape[1]
    width_local = resid.shape[2]
    width_all = width_local * n_chip * n_core
    feats_all = enc_w.shape[2]
    share = feats_all // (n_chip * n_core)
    other = 1 - core

    half = feats_all // n_core
    x = resid[0]
    we = enc_w[0]
    we_mine = lax.dynamic_slice_in_dim(we, core * half, half, 1)
    we_give = lax.dynamic_slice_in_dim(we, other * half, half, 1)
    we_got = lax.ppermute(we_give, "core", SWAP)
    x_got = lax.ppermute(x, "core", SWAP)
    pre = lax.dot_general(we_mine, x, (((0,), (1,)), ((), ())), preferred_element_type=jnp.float32)
    pre = pre + lax.dot_general(we_got, x_got, (((0,), (1,)), ((), ())), preferred_element_type=jnp.float32)
    n_x = lax.axis_size("wx")
    n_z = lax.axis_size("wz")
    pre_x = lax.psum_scatter(pre, "wx", scatter_dimension=0, tiled=True)
    pre_share = lax.psum_scatter(pre_x, "wz", scatter_dimension=0, tiled=True)
    block = core * n_chip + lax.axis_index("wx") * n_z + lax.axis_index("wz")
    bias = lax.dynamic_slice_in_dim(enc_b[0], block * share, share, 0)
    feats_t = jnp.maximum(pre_share + bias[:, None], 0.0).astype(jnp.bfloat16)
    feats = lax.all_gather(feats_t, WIDTH, axis=0, tiled=True)
    wd = dec_w[0].reshape(n_core, n_x, n_z, share, width_local).transpose(2, 1, 0, 3, 4)
    wd = wd.reshape(feats_all, width_local)
    mlp_cols = contract0(wd, feats)

    query_rows = rows_all // n_src
    row_start = src * query_rows
    mlp_blocks = mlp_cols.reshape(width_local, n_src, query_rows).transpose(1, 0, 2)
    mlp = halving_sum(mlp_blocks, "src", n_src, src).T
    mlp_out = mlp.astype(jnp.bfloat16)
    tgt = lax.dynamic_slice_in_dim(target, row_start, query_rows, 0)
    stream = tgt.astype(jnp.float32) + mlp
    n_width = n_chip * n_core
    n_kv = wk.shape[1] // HD
    lifted = stream * norm_gain[None, :]
    exact = lax.Precision.HIGHEST
    key_part = jnp.dot(lifted, wk.astype(jnp.float32), precision=exact).reshape(query_rows, n_kv, 1, HD)
    value_part = jnp.dot(lifted, wv.astype(jnp.float32), precision=exact).reshape(query_rows, n_kv, 1, HD)
    kv_part = jnp.concatenate([key_part, value_part], axis=2).reshape(query_rows, n_kv * 2 * HD)
    head_cols = 2 * HD
    n_heads_kv = kv_part.shape[1] // head_cols
    kv_blocks = kv_part.reshape(query_rows, n_heads_kv, head_cols).transpose(1, 0, 2)
    row_power = jnp.sum(stream * stream, axis=1)
    power_col = jnp.broadcast_to(row_power[None, :, None], (n_heads_kv, query_rows, 1))
    kv_blocks = jnp.concatenate([kv_blocks, power_col], axis=2)
    w_bits = n_width.bit_length() - 1
    low_bits = w_bits - (n_heads_kv.bit_length() - 1)
    kv_sum = halving_bits(kv_blocks, WIDTH, n_width, width_pos, list(range(low_bits, w_bits)))
    for b in range(low_bits):
        kv_sum = kv_sum + lax.ppermute(kv_sum, WIDTH, [(i, i ^ (1 << b)) for i in range(n_width)])
    kv_scale = lax.rsqrt(kv_sum[:, head_cols] / width_all + 1e-05)[:, None]
    kv_head = (kv_sum[:, :head_cols] * kv_scale).astype(jnp.bfloat16)
    kv_all = doubling_gather(kv_head, "src", n_src, src).reshape(rows_all, head_cols)

    packed = jnp.concatenate([stream, norm_gain[None, :]], axis=0)
    packed_full = lax.all_gather(packed, WIDTH, axis=1, tiled=True)
    stream_full = packed_full[:query_rows]
    gain_full = packed_full[query_rows]
    power = jnp.sum(stream_full * stream_full, axis=1) / width_all
    scale = lax.rsqrt(power + 1e-05)[:, None]
    normed_full = (stream_full * scale * gain_full[None, :]).astype(jnp.bfloat16)
    query = jnp.dot(normed_full, wq, preferred_element_type=jnp.float32).astype(jnp.bfloat16)

    key_head = kv_all[:, :HD]
    value_head = kv_all[:, HD:]
    heads_here = wq.shape[1] // HD

    query3 = query.reshape(query_rows, heads_here, HD)
    scores = jnp.einsum(
        "qhd,sd->hqs", query3, key_head, preferred_element_type=jnp.float32
    ) / math.sqrt(HD)
    query_index = row_start + jnp.arange(query_rows, dtype=jnp.int32)
    key_index = jnp.arange(rows_all, dtype=jnp.int32)
    query_prompt = lax.dynamic_slice_in_dim(prompt_ids, row_start, query_rows, 0)
    allowed = (query_prompt[:, None] == prompt_ids[None, :]) & (
        key_index[None, :] <= query_index[:, None]
    )
    scores = jnp.where(allowed[None], scores, -1e30)
    peak = jnp.max(scores, axis=-1, keepdims=True)
    weights = jnp.exp(scores - peak)
    probs = (weights / jnp.sum(weights, axis=-1, keepdims=True)).astype(jnp.bfloat16)
    context = jnp.einsum("hqs,sd->qhd", probs, value_head, preferred_element_type=jnp.float32)
    return (mlp_out, context.reshape(query_rows, heads_here * HD).astype(jnp.bfloat16))


def solution(mesh):
    n_src = mesh.shape["src"]
    n_width = mesh.shape["width"]
    fine = Mesh(mesh.devices.reshape(n_src, n_width // 8, 4, 2), ("src", "wz", "wx", "core"))
    in_specs = (
        P("src", None, WIDTH),
        P("src", WIDTH, None),
        P("src", None),
        P("src", None, WIDTH),
        P(None, WIDTH),
        P(WIDTH),
        P(None, WIDTH),
        P(WIDTH, None),
        P(WIDTH, None),
        P(),
    )
    out_specs = (P("src", WIDTH), P("src", WIDTH))
    return jax.shard_map(
        on_device, mesh=fine, in_specs=in_specs, out_specs=out_specs, check_vma=False
    )
```

```python
import math

import jax
import jax.numpy as jnp
from jax import lax
from jax.sharding import Mesh
from jax.sharding import PartitionSpec as P


HD = 128
WIDTH = ("wch", "wcl", "core")
CHIP = ("wch", "wcl")
SWAP = [(0, 1), (1, 0)]


def contract0(a, b):
    return lax.dot_general(a, b, (((0,), (0,)), ((), ())), preferred_element_type=jnp.float32)


def halving_sum(blocks, axis, n, me):
    bits = n.bit_length() - 1
    rest = blocks.shape[1:]
    cur = blocks.reshape((2,) * bits + rest)
    for b in range(bits):
        ax = bits - 1 - b
        mine_bit = (me >> b) & 1
        keep = lax.dynamic_index_in_dim(cur, mine_bit, ax, keepdims=False)
        give = lax.dynamic_index_in_dim(cur, 1 - mine_bit, ax, keepdims=False)
        cur = keep + lax.ppermute(give, axis, [(i, i ^ (1 << b)) for i in range(n)])
    return cur


def halving_bits(blocks, axis, n, me, flips):
    kbits = len(flips)
    rest = blocks.shape[1:]
    cur = blocks.reshape((2,) * kbits + rest)
    for k in range(kbits):
        ax = kbits - 1 - k
        mine_bit = (me >> flips[k]) & 1
        keep = lax.dynamic_index_in_dim(cur, mine_bit, ax, keepdims=False)
        give = lax.dynamic_index_in_dim(cur, 1 - mine_bit, ax, keepdims=False)
        cur = keep + lax.ppermute(give, axis, [(i, i ^ (1 << flips[k])) for i in range(n)])
    return cur


def doubling_gather(piece, axis, n, me):
    bits = n.bit_length() - 1
    cur = piece
    for b in range(bits):
        got = lax.ppermute(cur, axis, [(i, i ^ (1 << b)) for i in range(n)])
        low = ((me >> b) & 1) == 0
        cur = jnp.where(low, jnp.stack([cur, got]), jnp.stack([got, cur]))
    return cur.reshape((n,) + piece.shape)


def on_device_body(resid, enc_w, enc_b, dec_w, target, norm_gain, wq, wk, wv, prompt_ids):
    n_chip = lax.axis_size(CHIP)
    n_core = lax.axis_size("core")
    n_src = lax.axis_size("src")
    core = lax.axis_index("core")
    chip = lax.axis_index(CHIP)
    src = lax.axis_index("src")
    width_pos = chip * n_core + core
    rows_all = resid.shape[1]
    width_local = resid.shape[2]
    width_all = width_local * n_chip * n_core
    feats_all = enc_w.shape[2]
    share = feats_all // (n_chip * n_core)
    other = 1 - core

    half = feats_all // n_core
    x = resid[0]
    we = enc_w[0]
    we_mine = lax.dynamic_slice_in_dim(we, core * half, half, 1)
    we_give = lax.dynamic_slice_in_dim(we, other * half, half, 1)
    we_got = lax.ppermute(we_give, "core", SWAP)
    x_got = lax.ppermute(x, "core", SWAP)
    pre = lax.dot_general(we_mine, x, (((0,), (1,)), ((), ())), preferred_element_type=jnp.float32)
    pre = pre + lax.dot_general(we_got, x_got, (((0,), (1,)), ((), ())), preferred_element_type=jnp.float32)
    pre_share = lax.psum_scatter(pre, CHIP, scatter_dimension=0, tiled=True)
    bias = lax.dynamic_slice_in_dim(enc_b[0], (core * n_chip + chip) * share, share, 0)
    feats_t = jnp.maximum(pre_share + bias[:, None], 0.0).astype(jnp.bfloat16)
    feats = lax.all_gather(feats_t, WIDTH, axis=0, tiled=True)
    wd = dec_w[0].reshape(n_core, n_chip, share, width_local).transpose(1, 0, 2, 3)
    wd = wd.reshape(feats_all, width_local)
    mlp_cols = contract0(wd, feats)

    query_rows = rows_all // n_src
    row_start = src * query_rows
    mlp_blocks = mlp_cols.reshape(width_local, n_src, query_rows).transpose(1, 0, 2)
    mlp = halving_sum(mlp_blocks, "src", n_src, src).T
    mlp_out = mlp.astype(jnp.bfloat16)
    tgt = lax.dynamic_slice_in_dim(target, row_start, query_rows, 0)
    stream = tgt.astype(jnp.float32) + mlp
    n_width = n_chip * n_core
    n_kv = wk.shape[1] // HD
    lifted = stream * norm_gain[None, :]
    exact = lax.Precision.HIGHEST
    key_part = jnp.dot(lifted, wk.astype(jnp.float32), precision=exact).reshape(query_rows, n_kv, 1, HD)
    value_part = jnp.dot(lifted, wv.astype(jnp.float32), precision=exact).reshape(query_rows, n_kv, 1, HD)
    kv_part = jnp.concatenate([key_part, value_part], axis=2).reshape(query_rows, n_kv * 2 * HD)
    head_cols = 2 * HD
    n_heads_kv = kv_part.shape[1] // head_cols
    kv_blocks = kv_part.reshape(query_rows, n_heads_kv, head_cols).transpose(1, 0, 2)
    row_power = jnp.sum(stream * stream, axis=1)
    power_col = jnp.broadcast_to(row_power[None, :, None], (n_heads_kv, query_rows, 1))
    kv_blocks = jnp.concatenate([kv_blocks, power_col], axis=2)
    w_bits = n_width.bit_length() - 1
    low_bits = w_bits - (n_heads_kv.bit_length() - 1)
    kv_sum = halving_bits(kv_blocks, WIDTH, n_width, width_pos, list(range(low_bits, w_bits)))
    for b in range(low_bits):
        kv_sum = kv_sum + lax.ppermute(kv_sum, WIDTH, [(i, i ^ (1 << b)) for i in range(n_width)])
    kv_scale = lax.rsqrt(kv_sum[:, head_cols] / width_all + 1e-05)[:, None]
    kv_head = (kv_sum[:, :head_cols] * kv_scale).astype(jnp.bfloat16)
    kv_all = doubling_gather(kv_head, "src", n_src, src).reshape(rows_all, head_cols)

    packed = jnp.concatenate([stream, norm_gain[None, :]], axis=0)
    packed_full = lax.all_gather(packed, WIDTH, axis=1, tiled=True)
    stream_full = packed_full[:query_rows]
    gain_full = packed_full[query_rows]
    power = jnp.sum(stream_full * stream_full, axis=1) / width_all
    scale = lax.rsqrt(power + 1e-05)[:, None]
    normed_full = (stream_full * scale * gain_full[None, :]).astype(jnp.bfloat16)
    query = jnp.dot(normed_full, wq, preferred_element_type=jnp.float32).astype(jnp.bfloat16)

    key_head = kv_all[:, :HD]
    value_head = kv_all[:, HD:]
    heads_here = wq.shape[1] // HD

    query3 = query.reshape(query_rows, heads_here, HD)
    scores = jnp.einsum(
        "qhd,sd->hqs", query3, key_head, preferred_element_type=jnp.float32
    ) / math.sqrt(HD)
    query_index = row_start + jnp.arange(query_rows, dtype=jnp.int32)
    key_index = jnp.arange(rows_all, dtype=jnp.int32)
    query_prompt = lax.dynamic_slice_in_dim(prompt_ids, row_start, query_rows, 0)
    allowed = (query_prompt[:, None] == prompt_ids[None, :]) & (
        key_index[None, :] <= query_index[:, None]
    )
    scores = jnp.where(allowed[None], scores, -1e30)
    peak = jnp.max(scores, axis=-1, keepdims=True)
    weights = jnp.exp(scores - peak)
    probs = (weights / jnp.sum(weights, axis=-1, keepdims=True)).astype(jnp.bfloat16)
    context = jnp.einsum("hqs,sd->qhd", probs, value_head, preferred_element_type=jnp.float32)
    return (mlp_out, context.reshape(query_rows, heads_here * HD).astype(jnp.bfloat16))


def solution(mesh):
    n_src = mesh.shape["src"]
    n_width = mesh.shape["width"]
    fine = Mesh(mesh.devices.reshape(n_src, n_width // 4, 2, 2), ("src", "wch", "wcl", "core"))
    in_specs = (
        P("src", None, WIDTH),
        P("src", WIDTH, None),
        P("src", None),
        P("src", None, WIDTH),
        P(None, WIDTH),
        P(WIDTH),
        P(None, WIDTH),
        P(WIDTH, None),
        P(WIDTH, None),
        P(),
    )
    out_specs = (P("src", WIDTH), P("src", WIDTH))
    return jax.shard_map(on_device_body, mesh=fine, in_specs=in_specs, out_specs=out_specs, check_vma=False)
```

```python
import math

import jax
import jax.numpy as jnp
from jax import lax
from jax.sharding import Mesh
from jax.sharding import PartitionSpec as P

HD = 128
GROUP = 8
WIDTH = ("wch", "wcl", "core")
CHIP = ("wch", "wcl")
SWAP = [(0, 1), (1, 0)]


def contract0(a, b):
    return lax.dot_general(a, b, (((0,), (0,)), ((), ())), preferred_element_type=jnp.float32)


def exchange_sum(blocks, axis, n, me):
    total = lax.dynamic_index_in_dim(blocks, me, 0, keepdims=False)
    for shift in range(1, n):
        piece = lax.dynamic_index_in_dim(blocks, (me + shift) % n, 0, keepdims=False)
        total = total + lax.ppermute(piece, axis, [(i, (i + shift) % n) for i in range(n)])
    return total


def halving_sum(blocks, axis, n, me):
    bits = n.bit_length() - 1
    rest = blocks.shape[1:]
    cur = blocks.reshape((2,) * bits + rest)
    for b in range(bits):
        ax = bits - 1 - b
        mine_bit = (me >> b) & 1
        keep = lax.dynamic_index_in_dim(cur, mine_bit, ax, keepdims=False)
        give = lax.dynamic_index_in_dim(cur, 1 - mine_bit, ax, keepdims=False)
        cur = keep + lax.ppermute(give, axis, [(i, i ^ (1 << b)) for i in range(n)])
    return cur


def halving_bits(blocks, axis, n, me, flips):
    kbits = len(flips)
    rest = blocks.shape[1:]
    cur = blocks.reshape((2,) * kbits + rest)
    for k in range(kbits):
        ax = kbits - 1 - k
        mine_bit = (me >> flips[k]) & 1
        keep = lax.dynamic_index_in_dim(cur, mine_bit, ax, keepdims=False)
        give = lax.dynamic_index_in_dim(cur, 1 - mine_bit, ax, keepdims=False)
        cur = keep + lax.ppermute(give, axis, [(i, i ^ (1 << flips[k])) for i in range(n)])
    return cur


def doubling_gather(piece, axis, n, me):
    bits = n.bit_length() - 1
    cur = piece
    for b in range(bits):
        got = lax.ppermute(cur, axis, [(i, i ^ (1 << b)) for i in range(n)])
        low = ((me >> b) & 1) == 0
        cur = jnp.where(low, jnp.stack([cur, got]), jnp.stack([got, cur]))
    return cur.reshape((n,) + piece.shape)


def on_device(resid, enc_w, enc_b, dec_w, target, norm_gain, wq, wk, wv, prompt_ids):
    n_chip = lax.axis_size(CHIP)
    n_core = lax.axis_size("core")
    n_src = lax.axis_size("src")
    core = lax.axis_index("core")
    chip = lax.axis_index(CHIP)
    src = lax.axis_index("src")
    width_pos = chip * n_core + core
    rows_all = resid.shape[1]
    width_local = resid.shape[2]
    width_all = width_local * n_chip * n_core
    feats_all = enc_w.shape[2]
    share = feats_all // (n_chip * n_core)
    other = 1 - core

    half = feats_all // n_core
    x = resid[0]
    we = enc_w[0]
    we_mine = lax.dynamic_slice_in_dim(we, core * half, half, 1)
    we_give = lax.dynamic_slice_in_dim(we, other * half, half, 1)
    we_got = lax.ppermute(we_give, "core", SWAP)
    x_got = lax.ppermute(x, "core", SWAP)
    pre = lax.dot_general(we_mine, x, (((0,), (1,)), ((), ())), preferred_element_type=jnp.float32)
    pre = pre + lax.dot_general(we_got, x_got, (((0,), (1,)), ((), ())), preferred_element_type=jnp.float32)
    pre_share = lax.psum_scatter(pre, CHIP, scatter_dimension=0, tiled=True)
    bias = lax.dynamic_slice_in_dim(enc_b[0], (core * n_chip + chip) * share, share, 0)
    feats_t = jnp.maximum(pre_share + bias[:, None], 0.0).astype(jnp.bfloat16)
    feats = lax.all_gather(feats_t, WIDTH, axis=0, tiled=True)
    wd = dec_w[0].reshape(n_core, n_chip, share, width_local)
    feats4 = feats.reshape(n_chip, n_core, share, rows_all)
    mlp_cols = lax.dot_general(
        wd, feats4, (((1, 0, 2), (0, 1, 2)), ((), ())), preferred_element_type=jnp.float32
    )

    query_rows = rows_all // n_src
    row_start = src * query_rows
    mlp_blocks = mlp_cols.reshape(width_local, n_src, query_rows).transpose(1, 0, 2)
    mlp = halving_sum(mlp_blocks, "src", n_src, src).T
    mlp_out = mlp.astype(jnp.bfloat16)
    tgt = lax.dynamic_slice_in_dim(target, row_start, query_rows, 0)
    stream = tgt.astype(jnp.float32) + mlp
    n_width = n_chip * n_core
    n_kv = wk.shape[1] // HD
    lifted = stream * norm_gain[None, :]
    exact = lax.Precision.HIGHEST
    key_part = jnp.dot(lifted, wk.astype(jnp.float32), precision=exact).reshape(query_rows, n_kv, 1, HD)
    value_part = jnp.dot(lifted, wv.astype(jnp.float32), precision=exact).reshape(query_rows, n_kv, 1, HD)
    kv_part = jnp.concatenate([key_part, value_part], axis=2).reshape(query_rows, n_kv * 2 * HD)
    head_cols = 2 * HD
    n_heads_kv = kv_part.shape[1] // head_cols
    kv_blocks = kv_part.reshape(query_rows, n_heads_kv, head_cols).transpose(1, 0, 2)
    row_power = jnp.sum(stream * stream, axis=1)
    power_col = jnp.broadcast_to(row_power[None, :, None], (n_heads_kv, query_rows, 1))
    kv_blocks = jnp.concatenate([kv_blocks, power_col], axis=2)
    w_bits = n_width.bit_length() - 1
    low_bits = w_bits - (n_heads_kv.bit_length() - 1)
    kv_sum = halving_bits(kv_blocks, WIDTH, n_width, width_pos, list(range(low_bits, w_bits)))
    for b in range(low_bits):
        kv_sum = kv_sum + lax.ppermute(kv_sum, WIDTH, [(i, i ^ (1 << b)) for i in range(n_width)])
    kv_scale = lax.rsqrt(kv_sum[:, head_cols] / width_all + 1e-05)[:, None]
    kv_head = (kv_sum[:, :head_cols] * kv_scale).astype(jnp.bfloat16)
    kv_all = doubling_gather(kv_head, "src", n_src, src).reshape(rows_all, head_cols)

    packed = jnp.concatenate([stream, norm_gain[None, :]], axis=0)
    packed_full = lax.all_gather(packed, WIDTH, axis=1, tiled=True)
    stream_full = packed_full[:query_rows]
    gain_full = packed_full[query_rows]
    power = jnp.sum(stream_full * stream_full, axis=1) / width_all
    scale = lax.rsqrt(power + 1e-05)[:, None]
    normed_full = (stream_full * scale * gain_full[None, :]).astype(jnp.bfloat16)
    query = jnp.dot(normed_full, wq, preferred_element_type=jnp.float32).astype(jnp.bfloat16)

    key_head = kv_all[:, :HD]
    value_head = kv_all[:, HD:]
    heads_here = wq.shape[1] // HD

    query3 = query.reshape(query_rows, heads_here, HD)
    scores = jnp.einsum(
        "qhd,sd->hqs", query3, key_head, preferred_element_type=jnp.float32
    ) / math.sqrt(HD)
    query_index = row_start + jnp.arange(query_rows, dtype=jnp.int32)
    key_index = jnp.arange(rows_all, dtype=jnp.int32)
    query_prompt = lax.dynamic_slice_in_dim(prompt_ids, row_start, query_rows, 0)
    allowed = (query_prompt[:, None] == prompt_ids[None, :]) & (
        key_index[None, :] <= query_index[:, None]
    )
    scores = jnp.where(allowed[None], scores, -1e30)
    peak = jnp.max(scores, axis=-1, keepdims=True)
    weights = jnp.exp(scores - peak)
    probs = (weights / jnp.sum(weights, axis=-1, keepdims=True)).astype(jnp.bfloat16)
    context = jnp.einsum("hqs,sd->qhd", probs, value_head, preferred_element_type=jnp.float32)
    return (mlp_out, context.reshape(query_rows, heads_here * HD).astype(jnp.bfloat16))


def solution(mesh):
    n_src = mesh.shape["src"]
    n_width = mesh.shape["width"]
    fine = Mesh(mesh.devices.reshape(n_src, n_width // 4, 2, 2), ("src", "wch", "wcl", "core"))
    in_specs = (
        P("src", None, WIDTH),
        P("src", WIDTH, None),
        P("src", None),
        P("src", None, WIDTH),
        P(None, WIDTH),
        P(WIDTH),
        P(None, WIDTH),
        P(WIDTH, None),
        P(WIDTH, None),
        P(),
    )
    out_specs = (P("src", WIDTH), P("src", WIDTH))
    return jax.shard_map(
        on_device, mesh=fine, in_specs=in_specs, out_specs=out_specs, check_vma=False
    )
```
